32 devices in a mesh: groups: 2 (over y), paths: 4 (over z), cols: 2 (over x), depth: 2 (over core).
Axes of the slice: x: 2, y: 2, z: 4, core: 2. Of those that a mesh axis runs over, the one named last changes fastest.
Arguments:
- panels: bfloat16 [96, 64, 1024], P(('groups', 'cols', 'paths'), None, 'depth'), parts along dimension 0, may hold values from -0.0546875 to 0.0546875
- model: bfloat16 [96, 1024], P(('groups', 'cols', 'paths'), 'depth'), parts along dimension 0, may hold values from -6 to 6
- depth_weight: bfloat16 [2048, 1024], P(('groups', 'paths'), 'depth'), parts along dimension 0, may hold values from -6 to 6
- seg_len: bfloat16 [2048, 48], P(('groups', 'paths'), 'cols'), parts along dimension 0, may hold values from 0.29882812 to 3
- path_start: int32 [2048], P(('groups', 'paths')), parts along dimension 0, may hold values from 0 to 47, as said below
- path_end: int32 [2048], P(('groups', 'paths')), parts along dimension 0, may hold values from 1 to 48, as said below
- mode_index: int32 [2048, 4], P(('groups', 'paths')), parts along dimension 0, may hold values from 0 to 63, all different within a row
- observed: float32 [2048, 4], P(('groups', 'paths')), parts along dimension 0, may hold values from -6 to 6
Outputs:
- gradient: float32 [96, 1024], P(('groups', 'cols', 'paths'), 'depth'), parts along dimension 0
- misfit: float32 [2048, 4], P(('groups', 'paths')), parts along dimension 0
The draws below stay inside these ranges and needn't reach their ends.
There are 2 independent parts, one for each index of `groups`. The reference program is written for one: setup_inputs(seed, part) draws one part's arguments, and reference() takes and returns one part's arrays. A program takes and returns all parts, laid end to end along the dimension named above; each array names one. Nothing has to cross between parts.
Inputs may be any that keep to these rules, and one draw needn't show every extreme that they name: `path_start`: each path starts before it ends; path 0 spans all 48 columns. `path_end`: each path ends after it starts. `mode_index`: each path names 4 different modes.
All inputs are finite; a program needn't handle non-finite values.
Results may differ from the reference program's by a relative error of at most 0.011.
Values may be sent and summed in bfloat16 or wider, within the bound.
No kernel may reach another device: no remote copies, remote signals or barrier semaphores. Data moves between devices by JAX's collectives and lax.ppermute only.
A program may use at most 64 MiB of HBM per device.

```python
import math
import jax
import jax.numpy as jnp
from jax import lax

M = 64
Z = 1024
KM = 4
COL_DEV = 6
P_SIZE = 1024
C = 48


def column_pair(key):
    first_draw = jax.random.randint(jax.random.fold_in(key, 11), (P_SIZE,), 0, C)
    second_draw = jax.random.randint(jax.random.fold_in(key, 12), (P_SIZE,), 0, C)
    lower = jnp.minimum(first_draw, second_draw)
    upper = jnp.maximum(first_draw, second_draw) + 1
    lower = lower.at[0].set(0)
    upper = upper.at[0].set(C)
    return (lower.astype(jnp.int32), upper.astype(jnp.int32))


def draw_path_start(key, part):
    return column_pair(key)[0]


def draw_path_end(key, part):
    return column_pair(key)[1]


def steps_of(key, extent, pieces, smallest, largest):
    loudness, own = 1.0, jax.random.fold_in(key, 6)
    for axis_at, shards_of in pieces:
        steps = jnp.exp(jax.random.uniform(jax.random.fold_in(own, axis_at), (shards_of,), jnp.float32, smallest / len(pieces), largest / len(pieces)))
        loudness = loudness * jnp.repeat(steps, extent[axis_at] // shards_of).reshape([-1 if axis == axis_at else 1 for axis in range(len(extent))])
    return loudness


def picks_of(key, rows, count, top, lift):
    ranking = jax.random.permutation(jax.random.fold_in(key, 1), count)
    boost = ranking
    for power in range(3):
        boost = boost * boost // count
    boost = boost * lift // count
    tickets = jax.random.randint(jax.random.fold_in(key, 2), (rows, count), 0, 4096) + boost
    holders = jax.random.permutation(jax.random.fold_in(key, 3), rows)[jnp.arange(count) % rows]
    tickets = jnp.where(jnp.arange(rows)[:, None] == holders[None, :], 1 << 14, tickets)
    score = tickets * count + jnp.arange(count)
    return lax.top_k(score.astype(jnp.int32), top)[1].astype(jnp.int32)


def gaussian(key, shape, scale, reach, split=(), kind=jnp.bfloat16):
    drawn = scale * jax.random.normal(key, shape, jnp.float32)
    if split:
        drawn = drawn * steps_of(key, shape, split, -0.22, 0.18)
    return jnp.clip(drawn, -reach, reach).astype(kind)


def setup_inputs(seed: int = 0, part: int = 0) -> dict:
    seeds = jax.random.split(jax.random.key(seed), 9)
    part_keys = jax.random.split(jax.random.fold_in(seeds[8], part), 9)
    panels = gaussian(part_keys[0], (C, M, Z), (C * Z // 4) ** -0.5, 0.0546875, ((0, 8), (2, 2)))
    model = gaussian(part_keys[1], (C, Z), 1.0, 6.0, ((0, 8), (1, 2)))
    depth_weight = gaussian(part_keys[2], (P_SIZE, Z), 1.0, 6.0, ((0, 4), (1, 2)))
    seg_len = jnp.clip(jnp.exp(math.log(3.0) - 2.306499 * jax.random.uniform(part_keys[3], (P_SIZE, C), jnp.float32) ** steps_of(part_keys[3], (P_SIZE, C), ((0, 4), (1, 2)), -0.2, 0.2)), 0.29882812, 3.0).astype(jnp.bfloat16)
    path_start = draw_path_start(jax.random.fold_in(jax.random.fold_in(seeds[8], part), 71), part)
    path_end = draw_path_end(jax.random.fold_in(jax.random.fold_in(seeds[8], part), 71), part)
    mode_index = picks_of(part_keys[6], P_SIZE, M, KM, 0)
    observed = gaussian(part_keys[7], (P_SIZE, KM), 1.0, 6.0, ((0, 4),), jnp.float32)
    return {"panels": panels, "model": model, "depth_weight": depth_weight, "seg_len": seg_len, "path_start": path_start, "path_end": path_end, "mode_index": mode_index, "observed": observed}


def reference(panels, model, depth_weight, seg_len, path_start, path_end, mode_index, observed):
    columns = jnp.arange(C, dtype=jnp.int32)
    inside = (columns[None, :] >= path_start[:, None]) & (columns[None, :] < path_end[:, None])
    lengths = jnp.where(inside, seg_len, jnp.zeros_like(seg_len))
    scaled = (panels.astype(jnp.float32) * model.astype(jnp.float32)[:, None, :]).astype(jnp.bfloat16)
    block_count = C // COL_DEV

    def forward_block(running, block_index):
        first_col = (block_index * COL_DEV).astype(jnp.int32)
        part_scaled = lax.dynamic_slice_in_dim(scaled, first_col, COL_DEV, 0).reshape(COL_DEV * M, Z)
        weighted = lax.dot_general(depth_weight, part_scaled, (((1,), (1,)), ((), ())), preferred_element_type=jnp.float32).reshape(P_SIZE, COL_DEV, M)
        row_weights = lax.dynamic_slice_in_dim(lengths, first_col, COL_DEV, 1).astype(jnp.float32)
        return running + jnp.einsum('pc,pcm->pm', row_weights, weighted), None

    travel, _ = lax.scan(forward_block, jnp.zeros((P_SIZE, M), jnp.float32), jnp.arange(block_count, dtype=jnp.int32))
    one_hot = (mode_index[:, :, None] == jnp.arange(M, dtype=jnp.int32)[None, None, :]).astype(jnp.float32)
    misfit = jnp.einsum('pkm,pm->pk', one_hot, travel) - observed
    resid_modes = jnp.einsum('pk,pkm->pm', misfit, one_hot)

    def backward_block(block_index):
        first_col = (block_index * COL_DEV).astype(jnp.int32)
        row_weights = lax.dynamic_slice_in_dim(lengths, first_col, COL_DEV, 1).astype(jnp.float32)
        spread = (row_weights[:, :, None] * resid_modes[:, None, :]).astype(jnp.bfloat16).reshape(P_SIZE, COL_DEV * M)
        summed = lax.dot_general(spread, depth_weight, (((0,), (0,)), ((), ())), preferred_element_type=jnp.float32).reshape(COL_DEV, M, Z)
        kernel_piece = lax.dynamic_slice_in_dim(panels, first_col, COL_DEV, 0).astype(jnp.float32)
        return jnp.sum(summed * kernel_piece, axis=1)

    gradient = lax.map(backward_block, jnp.arange(block_count, dtype=jnp.int32)).reshape(C, Z)
    return gradient, misfit
```

```python
import jax
import jax.numpy as jnp
from jax import lax
from jax.sharding import PartitionSpec as P

GROUP_AXES = ("paths", "cols", "depth")


def shifted_copies(x, axes, count):
    copies = [x]
    for shift in range(1, count):
        perm = [(i, (i + shift) % count) for i in range(count)]
        copies.append(lax.ppermute(x, axes, perm))
    return copies


def exchange_sum(x, axes, count):
    me = lax.axis_index(axes)
    copies = jnp.stack(shifted_copies(x, axes, count))
    copies = jnp.take(copies, (me - lax.iota(jnp.int32, count)) % count, axis=0)
    return jnp.sum(copies, axis=0)


def make_shards(n_paths, n_cols, n_depth):
    group = n_cols * n_paths * n_depth

    def shards(panels, model, depth_weight, seg_len, path_start, path_end, mode_index, observed):
        own_cols, modes, depth_half = panels.shape
        path_rows, block_cols = seg_len.shape
        kept = mode_index.shape[1]
        f32, bf16 = jnp.float32, jnp.bfloat16
        p_idx = lax.axis_index("paths")
        c_idx = lax.axis_index("cols")
        d_idx = lax.axis_index("depth")

        columns = c_idx * block_cols + lax.iota(jnp.int32, block_cols)
        inside = (columns[None, :] >= path_start[:, None]) & (columns[None, :] < path_end[:, None])
        lengths = jnp.where(inside, seg_len, jnp.zeros_like(seg_len))

        n_len = path_rows * block_cols
        n_mi = path_rows * kept
        small = jnp.concatenate([lengths.reshape(-1), mode_index.astype(bf16).reshape(-1)])
        pad = (-small.shape[0]) % depth_half
        small = jnp.pad(small, (0, pad)).reshape(-1, depth_half)
        payload = jnp.concatenate([depth_weight, small], axis=0)
        blocks = shifted_copies(payload, "paths", n_paths)

        scaled = (panels.astype(f32) * model.astype(f32)[:, None, :]).astype(bf16)
        scaled = scaled.reshape(own_cols * modes, depth_half)
        mode_ids = lax.iota(jnp.int32, modes)

        unpacked = []
        parts = []
        for s, blk in enumerate(blocks):
            dw_b = blk[:path_rows]
            sm = blk[path_rows:].reshape(-1)
            len_b = sm[:n_len].reshape(path_rows, block_cols)
            mi_b = sm[n_len:n_len + n_mi].reshape(path_rows, kept).astype(jnp.int32)
            len_own = lax.dynamic_slice_in_dim(len_b, p_idx * own_cols, own_cols, axis=1).astype(f32)
            one_hot = (mi_b[:, :, None] == mode_ids[None, None, :]).astype(f32)
            unpacked.append((dw_b, len_own, one_hot))
            weighted = lax.dot_general(
                dw_b, scaled, (((1,), (1,)), ((), ())), preferred_element_type=f32
            ).reshape(path_rows, own_cols, modes)
            per_mode = jnp.sum(len_own[:, :, None] * weighted, axis=1)
            part = jnp.sum(one_hot * per_mode[:, None, :], axis=2)
            parts.append(part.T)
        first = (c_idx == 0) & (d_idx == 0)
        parts[0] = parts[0] - jnp.where(first, observed.T, jnp.zeros_like(observed.T))
        by_shift = jnp.stack(parts)
        order = (p_idx - lax.iota(jnp.int32, n_paths)) % n_paths
        canon = jnp.take(by_shift, order, axis=0)

        if group <= 16:
            misfit_all = exchange_sum(canon, GROUP_AXES, group)
        else:
            misfit_all = exchange_sum(canon, ("cols", "depth"), n_cols * n_depth)
            misfit_all = exchange_sum(misfit_all, "paths", n_paths)
        misfit = jnp.take(misfit_all, p_idx, axis=0).T

        mis_shift = jnp.take(misfit_all, order, axis=0)
        summed = None
        for s, (dw_b, len_own, one_hot) in enumerate(unpacked):
            resid = jnp.sum(mis_shift[s].T[:, :, None] * one_hot, axis=1)
            spread = (len_own[:, :, None] * resid[:, None, :]).astype(bf16)
            spread = spread.reshape(path_rows, own_cols * modes)
            term = lax.dot_general(
                spread, dw_b, (((0,), (0,)), ((), ())), preferred_element_type=f32
            )
            summed = term if summed is None else summed + term
        summed = summed.reshape(own_cols, modes, depth_half)
        gradient = jnp.sum(summed * panels.astype(f32), axis=1)
        return (gradient, misfit)

    return shards


def solution(mesh):
    shards = make_shards(mesh.shape["paths"], mesh.shape["cols"], mesh.shape["depth"])
    return jax.shard_map(
        shards,
        mesh=mesh,
        in_specs=(
            P(("groups", "cols", "paths"), None, "depth"),
            P(("groups", "cols", "paths"), "depth"),
            P(("groups", "paths"), "depth"),
            P(("groups", "paths"), "cols"),
            P(("groups", "paths")),
            P(("groups", "paths")),
            P(("groups", "paths"), None),
            P(("groups", "paths"), None),
        ),
        out_specs=(P(("groups", "cols", "paths"), "depth"), P(("groups", "paths"), None)),
        check_vma=False,
    )
```

```python
import jax
import jax.numpy as jnp
from jax import lax
from jax.sharding import PartitionSpec as P

GROUP_AXES = ("paths", "cols", "depth")


def shifted_copies(x, axes, count):
    copies = [x]
    for shift in range(1, count):
        perm = [(i, (i + shift) % count) for i in range(count)]
        copies.append(lax.ppermute(x, axes, perm))
    return copies


def exchange_sum(x, axes, count):
    me = lax.axis_index(axes)
    copies = jnp.stack(shifted_copies(x, axes, count))
    copies = jnp.take(copies, (me - lax.iota(jnp.int32, count)) % count, axis=0)
    return jnp.sum(copies, axis=0)


def butterfly_sum(x, axes, count):
    step = 1
    while step < count:
        perm = [(i, i ^ step) for i in range(count)]
        x = x + lax.ppermute(x, axes, perm)
        step *= 2
    return x


def make_shards(n_paths, n_cols, n_depth):
    group = n_cols * n_paths * n_depth

    def shards(panels, model, depth_weight, seg_len, path_start, path_end, mode_index, observed):
        own_cols, modes, depth_half = panels.shape
        path_rows, block_cols = seg_len.shape
        kept = mode_index.shape[1]
        f32, bf16 = jnp.float32, jnp.bfloat16
        p_idx = lax.axis_index("paths")
        c_idx = lax.axis_index("cols")
        d_idx = lax.axis_index("depth")

        columns = c_idx * block_cols + lax.iota(jnp.int32, block_cols)
        inside = (columns[None, :] >= path_start[:, None]) & (columns[None, :] < path_end[:, None])
        lengths = jnp.where(inside, seg_len, jnp.zeros_like(seg_len))

        n_len = path_rows * block_cols
        n_mi = path_rows * kept
        small = jnp.concatenate([lengths.reshape(-1), mode_index.astype(bf16).reshape(-1)])
        pad = (-small.shape[0]) % depth_half
        small = jnp.pad(small, (0, pad)).reshape(-1, depth_half)
        payload = jnp.concatenate([depth_weight, small], axis=0)
        blocks = shifted_copies(payload, "paths", n_paths)

        scaled = (panels.astype(f32) * model.astype(f32)[:, None, :]).astype(bf16)
        scaled = scaled.reshape(own_cols * modes, depth_half)
        mode_ids = lax.iota(jnp.int32, modes)

        unpacked = []
        parts = []
        for s, blk in enumerate(blocks):
            dw_b = blk[:path_rows]
            sm = blk[path_rows:].reshape(-1)
            len_b = sm[:n_len].reshape(path_rows, block_cols)
            mi_b = sm[n_len:n_len + n_mi].reshape(path_rows, kept).astype(jnp.int32)
            len_own = lax.dynamic_slice_in_dim(len_b, p_idx * own_cols, own_cols, axis=1).astype(f32)
            one_hot = (mi_b[:, :, None] == mode_ids[None, None, :]).astype(f32)
            unpacked.append((dw_b, len_own, one_hot))
            weighted = lax.dot_general(
                dw_b, scaled, (((1,), (1,)), ((), ())), preferred_element_type=f32
            ).reshape(path_rows, own_cols, modes)
            per_mode = jnp.sum(len_own[:, :, None] * weighted, axis=1)
            part = jnp.sum(one_hot * per_mode[:, None, :], axis=2)
            parts.append(part.T)
        first = (c_idx == 0) & (d_idx == 0)
        parts[0] = parts[0] - jnp.where(first, observed.T, jnp.zeros_like(observed.T))
        by_shift = jnp.stack(parts)
        order = (p_idx - lax.iota(jnp.int32, n_paths)) % n_paths
        canon = jnp.take(by_shift, order, axis=0)

        if group & (group - 1) == 0:
            misfit_all = butterfly_sum(canon, GROUP_AXES, group)
        else:
            misfit_all = exchange_sum(canon, ("cols", "depth"), n_cols * n_depth)
            misfit_all = exchange_sum(misfit_all, "paths", n_paths)
        misfit = jnp.take(misfit_all, p_idx, axis=0).T

        mis_shift = jnp.take(misfit_all, order, axis=0)
        summed = None
        for s, (dw_b, len_own, one_hot) in enumerate(unpacked):
            resid = jnp.sum(mis_shift[s].T[:, :, None] * one_hot, axis=1)
            spread = (len_own[:, :, None] * resid[:, None, :]).astype(bf16)
            spread = spread.reshape(path_rows, own_cols * modes)
            term = lax.dot_general(
                spread, dw_b, (((0,), (0,)), ((), ())), preferred_element_type=f32
            )
            summed = term if summed is None else summed + term
        summed = summed.reshape(own_cols, modes, depth_half)
        gradient = jnp.sum(summed * panels.astype(f32), axis=1)
        return (gradient, misfit)

    return shards


def solution(mesh):
    shards = make_shards(mesh.shape["paths"], mesh.shape["cols"], mesh.shape["depth"])
    return jax.shard_map(
        shards,
        mesh=mesh,
        in_specs=(
            P(("groups", "cols", "paths"), None, "depth"),
            P(("groups", "cols", "paths"), "depth"),
            P(("groups", "paths"), "depth"),
            P(("groups", "paths"), "cols"),
            P(("groups", "paths")),
            P(("groups", "paths")),
            P(("groups", "paths"), None),
            P(("groups", "paths"), None),
        ),
        out_specs=(P(("groups", "cols", "paths"), "depth"), P(("groups", "paths"), None)),
        check_vma=False,
    )
```

```python
import jax
import jax.numpy as jnp
from jax import lax
from jax.sharding import PartitionSpec as P

GROUP_AXES = ("paths", "cols", "depth")


def shifted_copies(x, axes, count):
    copies = [x]
    for shift in range(1, count):
        perm = [(i, (i + shift) % count) for i in range(count)]
        copies.append(lax.ppermute(x, axes, perm))
    return copies


def exchange_sum(x, axes, count):
    me = lax.axis_index(axes)
    copies = jnp.stack(shifted_copies(x, axes, count))
    copies = jnp.take(copies, (me - lax.iota(jnp.int32, count)) % count, axis=0)
    return jnp.sum(copies, axis=0)


def butterfly_sum(x, axes, count):
    step = 1
    while step < count:
        perm = [(i, i ^ step) for i in range(count)]
        x = x + lax.ppermute(x, axes, perm)
        step *= 2
    return x


def pack_rows(flat, width):
    pad = (-flat.shape[0]) % width
    return jnp.pad(flat, (0, pad)).reshape(-1, width)


def make_shards(n_paths, n_cols, n_depth):
    group = n_cols * n_paths * n_depth
    split = n_cols == 2

    def shards(panels, model, depth_weight, seg_len, path_start, path_end, mode_index, observed):
        own_cols, modes, depth_half = panels.shape
        path_rows, block_cols = seg_len.shape
        kept = mode_index.shape[1]
        f32, bf16 = jnp.float32, jnp.bfloat16
        p_idx = lax.axis_index("paths")
        c_idx = lax.axis_index("cols")
        d_idx = lax.axis_index("depth")

        columns = c_idx * block_cols + lax.iota(jnp.int32, block_cols)
        inside = (columns[None, :] >= path_start[:, None]) & (columns[None, :] < path_end[:, None])
        lengths = jnp.where(inside, seg_len, jnp.zeros_like(seg_len))
        n_len = path_rows * block_cols
        n_mi = path_rows * kept
        small_flat = jnp.concatenate([lengths.reshape(-1), mode_index.astype(bf16).reshape(-1)])

        scaled = (panels.astype(f32) * model.astype(f32)[:, None, :]).astype(bf16)
        scaled = scaled.reshape(own_cols * modes, depth_half)

        if split:
            width = depth_half // 2
            own_off = c_idx * width
            other_off = (1 - c_idx) * width
            offsets = [own_off, other_off]
            mine = lax.dynamic_slice_in_dim(depth_weight, own_off, width, axis=1)
            theirs = lax.dynamic_slice_in_dim(depth_weight, other_off, width, axis=1)
            payload = jnp.concatenate([mine, pack_rows(small_flat, width)], axis=0)
            z_copies = shifted_copies(payload, "paths", n_paths)
            blocks = [([mine, theirs], small_flat)]
            for s in range(1, n_paths):
                got = z_copies[s]
                half = got[:path_rows]
                across = lax.ppermute(half, "cols", [(0, 1), (1, 0)])
                blocks.append(([half, across], got[path_rows:].reshape(-1)))
        else:
            width = depth_half
            offsets = [0]
            payload = jnp.concatenate([depth_weight, pack_rows(small_flat, width)], axis=0)
            blocks = [
                ([got[:path_rows]], got[path_rows:].reshape(-1))
                for got in shifted_copies(payload, "paths", n_paths)
            ]
        scaled_parts = [lax.dynamic_slice_in_dim(scaled, off, width, axis=1) for off in offsets]
        mode_ids = lax.iota(jnp.int32, modes)

        unpacked = []
        parts = []
        for s, (dw_parts, sm) in enumerate(blocks):
            len_b = sm[:n_len].reshape(path_rows, block_cols)
            mi_b = sm[n_len:n_len + n_mi].reshape(path_rows, kept).astype(jnp.int32)
            len_own = lax.dynamic_slice_in_dim(len_b, p_idx * own_cols, own_cols, axis=1).astype(f32)
            one_hot = (mi_b[:, :, None] == mode_ids[None, None, :]).astype(f32)
            unpacked.append((dw_parts, len_own, one_hot))
            weighted = None
            for dw_part, sc_part in zip(dw_parts, scaled_parts):
                term = lax.dot_general(
                    dw_part, sc_part, (((1,), (1,)), ((), ())), preferred_element_type=f32
                )
                weighted = term if weighted is None else weighted + term
            weighted = weighted.reshape(path_rows, own_cols, modes)
            per_mode = jnp.sum(len_own[:, :, None] * weighted, axis=1)
            part = jnp.sum(one_hot * per_mode[:, None, :], axis=2)
            parts.append(part.T)
        first = (c_idx == 0) & (d_idx == 0)
        parts[0] = parts[0] - jnp.where(first, observed.T, jnp.zeros_like(observed.T))
        by_shift = jnp.stack(parts)
        order = (p_idx - lax.iota(jnp.int32, n_paths)) % n_paths
        canon = jnp.take(by_shift, order, axis=0)

        if group & (group - 1) == 0:
            misfit_all = butterfly_sum(canon, GROUP_AXES, group)
        else:
            misfit_all = exchange_sum(canon, ("cols", "depth"), n_cols * n_depth)
            misfit_all = exchange_sum(misfit_all, "paths", n_paths)
        misfit = jnp.take(misfit_all, p_idx, axis=0).T

        mis_shift = jnp.take(misfit_all, order, axis=0)
        summed = [None] * len(offsets)
        for s, (dw_parts, len_own, one_hot) in enumerate(unpacked):
            resid = jnp.sum(mis_shift[s].T[:, :, None] * one_hot, axis=1)
            spread = (len_own[:, :, None] * resid[:, None, :]).astype(bf16)
            spread = spread.reshape(path_rows, own_cols * modes)
            for j, dw_part in enumerate(dw_parts):
                term = lax.dot_general(
                    spread, dw_part, (((0,), (0,)), ((), ())), preferred_element_type=f32
                )
                summed[j] = term if summed[j] is None else summed[j] + term
        grads = []
        for acc, off in zip(summed, offsets):
            panel_part = lax.dynamic_slice_in_dim(panels, off, width, axis=2).astype(f32)
            grads.append(jnp.sum(acc.reshape(own_cols, modes, width) * panel_part, axis=1))
        if split:
            gradient = jnp.where(
                c_idx == 0,
                jnp.concatenate([grads[0], grads[1]], axis=1),
                jnp.concatenate([grads[1], grads[0]], axis=1),
            )
        else:
            gradient = grads[0]
        return (gradient, misfit)

    return shards


def solution(mesh):
    shards = make_shards(mesh.shape["paths"], mesh.shape["cols"], mesh.shape["depth"])
    return jax.shard_map(
        shards,
        mesh=mesh,
        in_specs=(
            P(("groups", "cols", "paths"), None, "depth"),
            P(("groups", "cols", "paths"), "depth"),
            P(("groups", "paths"), "depth"),
            P(("groups", "paths"), "cols"),
            P(("groups", "paths")),
            P(("groups", "paths")),
            P(("groups", "paths"), None),
            P(("groups", "paths"), None),
        ),
        out_specs=(P(("groups", "cols", "paths"), "depth"), P(("groups", "paths"), None)),
        check_vma=False,
    )
```

```python
import jax
import jax.numpy as jnp
from jax import lax
from jax.sharding import PartitionSpec as P

def shifted_copies(x, axes, count):
    copies = [x]
    for shift in range(1, count):
        perm = [(i, (i + shift) % count) for i in range(count)]
        copies.append(lax.ppermute(x, axes, perm))
    return copies


def place_by_source(copies, me, count):
    stacked = jnp.zeros((count,) + copies[0].shape, copies[0].dtype)
    for shift, piece in enumerate(copies):
        stacked = lax.dynamic_update_index_in_dim(stacked, piece, (me - shift) % count, 0)
    return stacked


def exchange_sum(x, axes, count):
    me = lax.axis_index(axes)
    return jnp.sum(place_by_source(shifted_copies(x, axes, count), me, count), axis=0)


def butterfly_sum(x, axes, count):
    step = 1
    while step < count:
        perm = [(i, i ^ step) for i in range(count)]
        x = x + lax.ppermute(x, axes, perm)
        step *= 2
    return x


def pack_rows(flat, width):
    pad = (-flat.shape[0]) % width
    return jnp.pad(flat, (0, pad)).reshape(-1, width)


def make_shards(n_paths, n_cols, n_depth):
    split = n_cols == 2

    def shards(panels, model, depth_weight, seg_len, path_start, path_end, mode_index, observed):
        own_cols, modes, depth_half = panels.shape
        path_rows, block_cols = seg_len.shape
        kept = mode_index.shape[1]
        f32, bf16 = jnp.float32, jnp.bfloat16
        p_idx = lax.axis_index("paths")
        c_idx = lax.axis_index("cols")
        d_idx = lax.axis_index("depth")

        columns = c_idx * block_cols + lax.iota(jnp.int32, block_cols)
        inside = (columns[None, :] >= path_start[:, None]) & (columns[None, :] < path_end[:, None])
        lengths = jnp.where(inside, seg_len, jnp.zeros_like(seg_len))
        n_len = path_rows * block_cols
        n_mi = path_rows * kept
        small_flat = jnp.concatenate([lengths.reshape(-1), mode_index.astype(bf16).reshape(-1)])

        scaled = (panels.astype(f32) * model.astype(f32)[:, None, :]).astype(bf16)
        scaled = scaled.reshape(own_cols * modes, depth_half)

        if split:
            width = depth_half // 2
            own_off = c_idx * width
            other_off = (1 - c_idx) * width
            offsets = [own_off, other_off]
            mine = lax.dynamic_slice_in_dim(depth_weight, own_off, width, axis=1)
            theirs = lax.dynamic_slice_in_dim(depth_weight, other_off, width, axis=1)
            payload = jnp.concatenate([mine, pack_rows(small_flat, width)], axis=0)
            z_copies = shifted_copies(payload, "paths", n_paths)
            blocks = [([mine, theirs], small_flat)]
            for s in range(1, n_paths):
                got = z_copies[s]
                half = got[:path_rows]
                across = lax.ppermute(half, "cols", [(0, 1), (1, 0)])
                blocks.append(([half, across], got[path_rows:].reshape(-1)))
        else:
            width = depth_half
            offsets = [0]
            payload = jnp.concatenate([depth_weight, pack_rows(small_flat, width)], axis=0)
            blocks = [
                ([got[:path_rows]], got[path_rows:].reshape(-1))
                for got in shifted_copies(payload, "paths", n_paths)
            ]
        scaled_parts = [lax.dynamic_slice_in_dim(scaled, off, width, axis=1) for off in offsets]
        mode_ids = lax.iota(jnp.int32, modes)

        unpacked = []
        parts = []
        for s, (dw_parts, sm) in enumerate(blocks):
            len_b = sm[:n_len].reshape(path_rows, block_cols)
            mi_b = sm[n_len:n_len + n_mi].reshape(path_rows, kept).astype(jnp.int32)
            len_own = lax.dynamic_slice_in_dim(len_b, p_idx * own_cols, own_cols, axis=1).astype(f32)
            one_hot = (mi_b[:, :, None] == mode_ids[None, None, :]).astype(f32)
            unpacked.append((dw_parts, len_own, one_hot))
            weighted = None
            for dw_part, sc_part in zip(dw_parts, scaled_parts):
                term = lax.dot_general(
                    dw_part, sc_part, (((1,), (1,)), ((), ())), preferred_element_type=f32
                )
                weighted = term if weighted is None else weighted + term
            weighted = weighted.reshape(path_rows, own_cols, modes)
            per_mode = jnp.sum(len_own[:, :, None] * weighted, axis=1)
            part = jnp.sum(one_hot * per_mode[:, None, :], axis=2)
            parts.append(part.T)
        first = (c_idx == 0) & (d_idx == 0)
        parts[0] = parts[0] - jnp.where(first, observed.T, jnp.zeros_like(observed.T))
        canon = place_by_source(parts, p_idx, n_paths)

        local = n_cols * n_depth
        if local & (local - 1) == 0:
            misfit_all = butterfly_sum(canon, ("cols", "depth"), local)
        else:
            misfit_all = exchange_sum(canon, ("cols", "depth"), local)
        misfit_all = exchange_sum(misfit_all, "paths", n_paths)
        misfit = lax.dynamic_index_in_dim(misfit_all, p_idx, 0, keepdims=False).T
        mis_shift = [
            lax.dynamic_index_in_dim(misfit_all, (p_idx - s) % n_paths, 0, keepdims=False)
            for s in range(n_paths)
        ]
        summed = [None] * len(offsets)
        for s, (dw_parts, len_own, one_hot) in enumerate(unpacked):
            resid = jnp.sum(mis_shift[s].T[:, :, None] * one_hot, axis=1)
            spread = (len_own[:, :, None] * resid[:, None, :]).astype(bf16)
            spread = spread.reshape(path_rows, own_cols * modes)
            for j, dw_part in enumerate(dw_parts):
                term = lax.dot_general(
                    spread, dw_part, (((0,), (0,)), ((), ())), preferred_element_type=f32
                )
                summed[j] = term if summed[j] is None else summed[j] + term
        grads = []
        for acc, off in zip(summed, offsets):
            panel_part = lax.dynamic_slice_in_dim(panels, off, width, axis=2).astype(f32)
            grads.append(jnp.sum(acc.reshape(own_cols, modes, width) * panel_part, axis=1))
        if split:
            gradient = jnp.where(
                c_idx == 0,
                jnp.concatenate([grads[0], grads[1]], axis=1),
                jnp.concatenate([grads[1], grads[0]], axis=1),
            )
        else:
            gradient = grads[0]
        return (gradient, misfit)

    return shards


def solution(mesh):
    shards = make_shards(mesh.shape["paths"], mesh.shape["cols"], mesh.shape["depth"])
    return jax.shard_map(
        shards,
        mesh=mesh,
        in_specs=(
            P(("groups", "cols", "paths"), None, "depth"),
            P(("groups", "cols", "paths"), "depth"),
            P(("groups", "paths"), "depth"),
            P(("groups", "paths"), "cols"),
            P(("groups", "paths")),
            P(("groups", "paths")),
            P(("groups", "paths"), None),
            P(("groups", "paths"), None),
        ),
        out_specs=(P(("groups", "cols", "paths"), "depth"), P(("groups", "paths"), None)),
        check_vma=False,
    )
```

```python
import jax
import jax.numpy as jnp
from jax import lax
from jax.sharding import PartitionSpec as P

def shifted_copies(x, axes, count):
    copies = [x]
    for shift in range(1, count):
        perm = [(i, (i + shift) % count) for i in range(count)]
        copies.append(lax.ppermute(x, axes, perm))
    return copies


def place_by_source(copies, me, count):
    stacked = jnp.zeros((count,) + copies[0].shape, copies[0].dtype)
    for shift, piece in enumerate(copies):
        stacked = lax.dynamic_update_index_in_dim(stacked, piece, (me - shift) % count, 0)
    return stacked


def exchange_sum(x, axes, count):
    me = lax.axis_index(axes)
    return jnp.sum(place_by_source(shifted_copies(x, axes, count), me, count), axis=0)


def butterfly_sum(x, axes, count):
    step = 1
    while step < count:
        perm = [(i, i ^ step) for i in range(count)]
        x = x + lax.ppermute(x, axes, perm)
        step *= 2
    return x


def pack_rows(flat, width):
    pad = (-flat.shape[0]) % width
    return jnp.pad(flat, (0, pad)).reshape(-1, width)


def make_shards(n_paths, n_cols, n_depth):
    split = n_cols == 2

    def shards(panels, model, depth_weight, seg_len, path_start, path_end, mode_index, observed):
        own_cols, modes, depth_half = panels.shape
        path_rows, block_cols = seg_len.shape
        kept = mode_index.shape[1]
        f32, bf16 = jnp.float32, jnp.bfloat16
        p_idx = lax.axis_index("paths")
        c_idx = lax.axis_index("cols")
        d_idx = lax.axis_index("depth")

        columns = c_idx * block_cols + lax.iota(jnp.int32, block_cols)
        inside = (columns[None, :] >= path_start[:, None]) & (columns[None, :] < path_end[:, None])
        lengths = jnp.where(inside, seg_len, jnp.zeros_like(seg_len))
        def small_for(target):
            cols_of = lax.dynamic_slice_in_dim(lengths, target * own_cols, own_cols, axis=1)
            return jnp.concatenate([cols_of.reshape(-1), mode_index.astype(bf16).reshape(-1)])

        n_len = path_rows * own_cols
        n_mi = path_rows * kept

        scaled = (panels.astype(f32) * model.astype(f32)[:, None, :]).astype(bf16)
        scaled = scaled.reshape(own_cols * modes, depth_half)

        if split:
            width = depth_half // 2
            own_off = c_idx * width
            other_off = (1 - c_idx) * width
            offsets = [own_off, other_off]
            mine = lax.dynamic_slice_in_dim(depth_weight, own_off, width, axis=1)
            theirs = lax.dynamic_slice_in_dim(depth_weight, other_off, width, axis=1)
            head = [mine]
        else:
            width = depth_half
            offsets = [0]
            head = [depth_weight]
        blocks = [(head + ([theirs] if split else []), small_for(p_idx))]
        for shift in range(1, n_paths):
            target = (p_idx + shift) % n_paths
            payload = jnp.concatenate([head[0], pack_rows(small_for(target), width)], axis=0)
            perm = [(i, (i + shift) % n_paths) for i in range(n_paths)]
            got = lax.ppermute(payload, "paths", perm)
            part_rows = got[:path_rows]
            dw_parts = [part_rows]
            if split:
                dw_parts.append(lax.ppermute(part_rows, "cols", [(0, 1), (1, 0)]))
            blocks.append((dw_parts, got[path_rows:].reshape(-1)))
        scaled_parts = [lax.dynamic_slice_in_dim(scaled, off, width, axis=1) for off in offsets]
        mode_ids = lax.iota(jnp.int32, modes)

        unpacked = []
        parts = []
        for s, (dw_parts, sm) in enumerate(blocks):
            len_own = sm[:n_len].reshape(path_rows, own_cols).astype(f32)
            mi_b = sm[n_len:n_len + n_mi].reshape(path_rows, kept).astype(jnp.int32)
            one_hot = (mi_b[:, :, None] == mode_ids[None, None, :]).astype(f32)
            unpacked.append((dw_parts, len_own, one_hot))
            weighted = None
            for dw_part, sc_part in zip(dw_parts, scaled_parts):
                term = lax.dot_general(
                    dw_part, sc_part, (((1,), (1,)), ((), ())), preferred_element_type=f32
                )
                weighted = term if weighted is None else weighted + term
            weighted = weighted.reshape(path_rows, own_cols, modes)
            per_mode = jnp.sum(len_own[:, :, None] * weighted, axis=1)
            part = jnp.sum(one_hot * per_mode[:, None, :], axis=2)
            parts.append(part.T)
        first = (c_idx == 0) & (d_idx == 0)
        parts[0] = parts[0] - jnp.where(first, observed.T, jnp.zeros_like(observed.T))
        canon = place_by_source(parts, p_idx, n_paths)

        local = n_cols * n_depth
        if local & (local - 1) == 0:
            misfit_all = butterfly_sum(canon, ("cols", "depth"), local)
        else:
            misfit_all = exchange_sum(canon, ("cols", "depth"), local)
        misfit_all = exchange_sum(misfit_all, "paths", n_paths)
        misfit = lax.dynamic_index_in_dim(misfit_all, p_idx, 0, keepdims=False).T
        mis_shift = [
            lax.dynamic_index_in_dim(misfit_all, (p_idx - s) % n_paths, 0, keepdims=False)
            for s in range(n_paths)
        ]
        summed = [None] * len(offsets)
        for s, (dw_parts, len_own, one_hot) in enumerate(unpacked):
            resid = jnp.sum(mis_shift[s].T[:, :, None] * one_hot, axis=1)
            spread = (len_own[:, :, None] * resid[:, None, :]).astype(bf16)
            spread = spread.reshape(path_rows, own_cols * modes)
            for j, dw_part in enumerate(dw_parts):
                term = lax.dot_general(
                    spread, dw_part, (((0,), (0,)), ((), ())), preferred_element_type=f32
                )
                summed[j] = term if summed[j] is None else summed[j] + term
        grads = []
        for acc, off in zip(summed, offsets):
            panel_part = lax.dynamic_slice_in_dim(panels, off, width, axis=2).astype(f32)
            grads.append(jnp.sum(acc.reshape(own_cols, modes, width) * panel_part, axis=1))
        gradient = jnp.zeros((own_cols, depth_half), f32)
        for g, off in zip(grads, offsets):
            gradient = lax.dynamic_update_slice_in_dim(gradient, g, off, axis=1)
        return (gradient, misfit)

    return shards


def solution(mesh):
    shards = make_shards(mesh.shape["paths"], mesh.shape["cols"], mesh.shape["depth"])
    return jax.shard_map(
        shards,
        mesh=mesh,
        in_specs=(
            P(("groups", "cols", "paths"), None, "depth"),
            P(("groups", "cols", "paths"), "depth"),
            P(("groups", "paths"), "depth"),
            P(("groups", "paths"), "cols"),
            P(("groups", "paths")),
            P(("groups", "paths")),
            P(("groups", "paths"), None),
            P(("groups", "paths"), None),
        ),
        out_specs=(P(("groups", "cols", "paths"), "depth"), P(("groups", "paths"), None)),
        check_vma=False,
    )
```

```python
import jax
import jax.numpy as jnp
from jax import lax
from jax.sharding import PartitionSpec as P


def shifted_copies(x, axes, count):
    copies = [x]
    for shift in range(1, count):
        perm = [(i, (i + shift) % count) for i in range(count)]
        copies.append(lax.ppermute(x, axes, perm))
    return copies


def place_by_source(copies, me, count):
    stacked = jnp.zeros((count,) + copies[0].shape, copies[0].dtype)
    for shift, piece in enumerate(copies):
        stacked = lax.dynamic_update_index_in_dim(stacked, piece, (me - shift) % count, 0)
    return stacked


def exchange_sum(x, axes, count):
    me = lax.axis_index(axes)
    return jnp.sum(place_by_source(shifted_copies(x, axes, count), me, count), axis=0)


def butterfly_sum(x, axes, count):
    step = 1
    while step < count:
        perm = [(i, i ^ step) for i in range(count)]
        x = x + lax.ppermute(x, axes, perm)
        step *= 2
    return x


def pack_rows(flat, width):
    pad = (-flat.shape[0]) % width
    return jnp.pad(flat, (0, pad)).reshape(-1, width)


def make_shards(n_paths, n_cols, n_depth):
    split = n_cols == 2

    def shards(panels, model, depth_weight, seg_len, path_start, path_end, mode_index, observed):
        own_cols, modes, depth_half = panels.shape
        path_rows, block_cols = seg_len.shape
        kept = mode_index.shape[1]
        f32, bf16 = jnp.float32, jnp.bfloat16
        p_idx = lax.axis_index("paths")
        c_idx = lax.axis_index("cols")
        d_idx = lax.axis_index("depth")

        columns = c_idx * block_cols + lax.iota(jnp.int32, block_cols)
        inside = (columns[None, :] >= path_start[:, None]) & (columns[None, :] < path_end[:, None])
        lengths = jnp.where(inside, seg_len, jnp.zeros_like(seg_len))

        def lengths_of(target):
            return lax.dynamic_slice_in_dim(lengths, target * own_cols, own_cols, axis=1)

        def small_for(target):
            return jnp.concatenate(
                [lengths_of(target).reshape(-1), mode_index.astype(bf16).reshape(-1)]
            )

        n_len = path_rows * own_cols
        n_mi = path_rows * kept
        n_sets = 2 if split else 1
        width = depth_half // n_sets

        def scale(pan, mod):
            return (pan.astype(f32) * mod.astype(f32)[:, None, :]).astype(bf16)

        if split:
            own_off = c_idx * width
            other_off = (1 - c_idx) * width
            head = lax.dynamic_slice_in_dim(depth_weight, own_off, width, axis=1)
            pan_out = lax.dynamic_slice_in_dim(panels, other_off, width, axis=2)
            mod_out = lax.dynamic_slice_in_dim(model, other_off, width, axis=1)
            x_msg = jnp.concatenate(
                [
                    pan_out.reshape(own_cols * modes, width),
                    mod_out,
                    pack_rows(lengths_of(p_idx).reshape(-1), width),
                ],
                axis=0,
            )
            x_got = lax.ppermute(x_msg, "cols", [(0, 1), (1, 0)])
            n_pan = own_cols * modes
            pan_nb = x_got[:n_pan].reshape(own_cols, modes, width)
            mod_nb = x_got[n_pan:n_pan + own_cols]
            len_nb_own = x_got[n_pan + own_cols:].reshape(-1)[:n_len].reshape(path_rows, own_cols)
            pan_mine = lax.dynamic_slice_in_dim(panels, own_off, width, axis=2)
            mod_mine = lax.dynamic_slice_in_dim(model, own_off, width, axis=1)
            col_panels = [pan_mine, pan_nb]
            scaled2 = jnp.concatenate([scale(pan_mine, mod_mine), scale(pan_nb, mod_nb)], axis=0)
            scaled2 = scaled2.reshape(n_sets * own_cols * modes, width)
        else:
            head = depth_weight
            col_panels = [panels]
            scaled2 = scale(panels, model).reshape(own_cols * modes, width)

        blocks = [(head, [lengths_of(p_idx)] + ([len_nb_own] if split else []), mode_index)]
        for shift in range(1, n_paths):
            target = (p_idx + shift) % n_paths
            payload = jnp.concatenate([head, pack_rows(small_for(target), width)], axis=0)
            perm = [(i, (i + shift) % n_paths) for i in range(n_paths)]
            got = lax.ppermute(payload, "paths", perm)
            sm = got[path_rows:].reshape(-1)
            lens = [sm[:n_len].reshape(path_rows, own_cols)]
            if split:
                diag = [
                    (q * n_cols + c, ((q + shift) % n_paths) * n_cols + (1 - c))
                    for q in range(n_paths)
                    for c in range(n_cols)
                ]
                lens.append(
                    lax.ppermute(pack_rows(lengths_of(target).reshape(-1), width), ("paths", "cols"), diag)
                    .reshape(-1)[:n_len]
                    .reshape(path_rows, own_cols)
                )
            mi_b = sm[n_len:n_len + n_mi].reshape(path_rows, kept).astype(jnp.int32)
            blocks.append((got[:path_rows], lens, mi_b))
        mode_ids = lax.iota(jnp.int32, modes)

        unpacked = []
        parts = []
        for s, (dw_b, lens, mi_b) in enumerate(blocks):
            len_all = jnp.concatenate(lens, axis=1).astype(f32)
            one_hot = (mi_b[:, :, None] == mode_ids[None, None, :]).astype(f32)
            unpacked.append((dw_b, len_all, one_hot))
            weighted = lax.dot_general(
                dw_b, scaled2, (((1,), (1,)), ((), ())), preferred_element_type=f32
            ).reshape(path_rows, n_sets * own_cols, modes)
            per_mode = jnp.sum(len_all[:, :, None] * weighted, axis=1)
            part = jnp.sum(one_hot * per_mode[:, None, :], axis=2)
            parts.append(part.T)
        first = (c_idx == 0) & (d_idx == 0)
        parts[0] = parts[0] - jnp.where(first, observed.T, jnp.zeros_like(observed.T))
        canon = place_by_source(parts, p_idx, n_paths)

        local = n_cols * n_depth
        if local & (local - 1) == 0:
            misfit_all = butterfly_sum(canon, ("cols", "depth"), local)
        else:
            misfit_all = exchange_sum(canon, ("cols", "depth"), local)
        misfit_all = exchange_sum(misfit_all, "paths", n_paths)
        misfit = lax.dynamic_index_in_dim(misfit_all, p_idx, 0, keepdims=False).T

        summed = None
        for s, (dw_b, len_all, one_hot) in enumerate(unpacked):
            mis_b = lax.dynamic_index_in_dim(misfit_all, (p_idx - s) % n_paths, 0, keepdims=False)
            resid = jnp.sum(mis_b.T[:, :, None] * one_hot, axis=1)
            spread = (len_all[:, :, None] * resid[:, None, :]).astype(bf16)
            spread = spread.reshape(path_rows, n_sets * own_cols * modes)
            term = lax.dot_general(
                spread, dw_b, (((0,), (0,)), ((), ())), preferred_element_type=f32
            )
            summed = term if summed is None else summed + term
        summed = summed.reshape(n_sets, own_cols, modes, width)
        grads = [
            jnp.sum(summed[j] * col_panels[j].astype(f32), axis=1) for j in range(n_sets)
        ]
        if split:
            back = lax.ppermute(grads[1], "cols", [(0, 1), (1, 0)])
            gradient = jnp.zeros((own_cols, depth_half), f32)
            gradient = lax.dynamic_update_slice_in_dim(gradient, grads[0], own_off, axis=1)
            gradient = lax.dynamic_update_slice_in_dim(gradient, back, other_off, axis=1)
        else:
            gradient = grads[0]
        return (gradient, misfit)

    return shards


def solution(mesh):
    shards = make_shards(mesh.shape["paths"], mesh.shape["cols"], mesh.shape["depth"])
    return jax.shard_map(
        shards,
        mesh=mesh,
        in_specs=(
            P(("groups", "cols", "paths"), None, "depth"),
            P(("groups", "cols", "paths"), "depth"),
            P(("groups", "paths"), "depth"),
            P(("groups", "paths"), "cols"),
            P(("groups", "paths")),
            P(("groups", "paths")),
            P(("groups", "paths"), None),
            P(("groups", "paths"), None),
        ),
        out_specs=(P(("groups", "cols", "paths"), "depth"), P(("groups", "paths"), None)),
        check_vma=False,
    )
```

```python
import jax
import jax.numpy as jnp
from jax import lax
from jax.sharding import PartitionSpec as P

def shifted_copies(x, axes, count):
    copies = [x]
    for shift in range(1, count):
        perm = [(i, (i + shift) % count) for i in range(count)]
        copies.append(lax.ppermute(x, axes, perm))
    return copies


def place_by_source(copies, me, count):
    stacked = jnp.zeros((count,) + copies[0].shape, copies[0].dtype)
    for shift, piece in enumerate(copies):
        stacked = lax.dynamic_update_index_in_dim(stacked, piece, (me - shift) % count, 0)
    return stacked


def exchange_sum(x, axes, count):
    me = lax.axis_index(axes)
    return jnp.sum(place_by_source(shifted_copies(x, axes, count), me, count), axis=0)


def butterfly_sum(x, axes, count):
    step = 1
    while step < count:
        perm = [(i, i ^ step) for i in range(count)]
        x = x + lax.ppermute(x, axes, perm)
        step *= 2
    return x


def pack_rows(flat, width):
    pad = (-flat.shape[0]) % width
    return jnp.pad(flat, (0, pad)).reshape(-1, width)


def make_shards(n_paths, n_cols, n_depth):
    split = n_cols == 2

    def shards(panels, model, depth_weight, seg_len, path_start, path_end, mode_index, observed):
        own_cols, modes, depth_half = panels.shape
        path_rows, block_cols = seg_len.shape
        kept = mode_index.shape[1]
        f32, bf16 = jnp.float32, jnp.bfloat16
        p_idx = lax.axis_index("paths")
        c_idx = lax.axis_index("cols")
        d_idx = lax.axis_index("depth")

        columns = c_idx * block_cols + lax.iota(jnp.int32, block_cols)
        inside = (columns[None, :] >= path_start[:, None]) & (columns[None, :] < path_end[:, None])
        lengths = jnp.where(inside, seg_len, jnp.zeros_like(seg_len))
        def small_for(target):
            cols_of = lax.dynamic_slice_in_dim(lengths, target * own_cols, own_cols, axis=1)
            return jnp.concatenate([cols_of.reshape(-1), mode_index.astype(bf16).reshape(-1)])

        n_len = path_rows * own_cols
        n_mi = path_rows * kept

        scaled = (panels.astype(f32) * model.astype(f32)[:, None, :]).astype(bf16)
        scaled = scaled.reshape(own_cols * modes, depth_half)

        if split:
            width = depth_half // 2
            own_off = c_idx * width
            other_off = (1 - c_idx) * width
            offsets = [own_off, other_off]
            mine = lax.dynamic_slice_in_dim(depth_weight, own_off, width, axis=1)
            theirs = lax.dynamic_slice_in_dim(depth_weight, other_off, width, axis=1)
            head = [mine]
        else:
            width = depth_half
            offsets = [0]
            head = [depth_weight]
        blocks = [(head + ([theirs] if split else []), small_for(p_idx))]
        for shift in range(1, n_paths):
            target = (p_idx + shift) % n_paths
            payload = jnp.concatenate([head[0], pack_rows(small_for(target), width)], axis=0)
            perm = [(i, (i + shift) % n_paths) for i in range(n_paths)]
            got = lax.ppermute(payload, "paths", perm)
            part_rows = got[:path_rows]
            dw_parts = [part_rows]
            if split:
                dw_parts.append(lax.ppermute(part_rows, "cols", [(0, 1), (1, 0)]))
            blocks.append((dw_parts, got[path_rows:].reshape(-1)))
        scaled_parts = [lax.dynamic_slice_in_dim(scaled, off, width, axis=1) for off in offsets]
        mode_ids = lax.iota(jnp.int32, modes)

        unpacked = []
        parts = []
        for s, (dw_parts, sm) in enumerate(blocks):
            len_own = sm[:n_len].reshape(path_rows, own_cols).astype(f32)
            mi_b = sm[n_len:n_len + n_mi].reshape(path_rows, kept).astype(jnp.int32)
            one_hot = (mi_b[:, :, None] == mode_ids[None, None, :]).astype(f32)
            unpacked.append((dw_parts, len_own, one_hot))
            weighted = None
            for dw_part, sc_part in zip(dw_parts, scaled_parts):
                term = lax.dot_general(
                    dw_part, sc_part, (((1,), (1,)), ((), ())), preferred_element_type=f32
                )
                weighted = term if weighted is None else weighted + term
            weighted = weighted.reshape(path_rows, own_cols, modes)
            per_mode = jnp.sum(len_own[:, :, None] * weighted, axis=1)
            part = jnp.sum(one_hot * per_mode[:, None, :], axis=2)
            parts.append(part.T)
        first = (c_idx == 0) & (d_idx == 0)
        parts[0] = parts[0] - jnp.where(first, observed.T, jnp.zeros_like(observed.T))
        canon = place_by_source(parts, p_idx, n_paths)

        local = n_cols * n_depth
        if local & (local - 1) == 0:
            misfit_all = butterfly_sum(canon, ("cols", "depth"), local)
        else:
            misfit_all = exchange_sum(canon, ("cols", "depth"), local)
        misfit_all = exchange_sum(misfit_all, "paths", n_paths)
        misfit = lax.dynamic_index_in_dim(misfit_all, p_idx, 0, keepdims=False).T
        rev = list(reversed(range(n_paths)))
        doubled = jnp.concatenate([misfit_all, misfit_all], axis=0)
        mis_rev = lax.dynamic_slice_in_dim(doubled, (p_idx + 1) % n_paths, n_paths, axis=0)
        mis_rows = jnp.swapaxes(mis_rev, 1, 2).reshape(n_paths * path_rows, kept)
        len_all = jnp.concatenate([unpacked[s][1] for s in rev], axis=0)
        hot_all = jnp.concatenate([unpacked[s][2] for s in rev], axis=0)
        resid = jnp.sum(mis_rows[:, :, None] * hot_all, axis=1)
        spread = (len_all[:, :, None] * resid[:, None, :]).astype(bf16)
        spread = spread.reshape(n_paths * path_rows, own_cols * modes)
        summed = []
        for j in range(len(offsets)):
            dw_all = jnp.concatenate([unpacked[s][0][j] for s in rev], axis=0)
            summed.append(
                lax.dot_general(
                    spread, dw_all, (((0,), (0,)), ((), ())), preferred_element_type=f32
                )
            )
        grads = []
        for acc, off in zip(summed, offsets):
            panel_part = lax.dynamic_slice_in_dim(panels, off, width, axis=2).astype(f32)
            grads.append(jnp.sum(acc.reshape(own_cols, modes, width) * panel_part, axis=1))
        gradient = jnp.zeros((own_cols, depth_half), f32)
        for g, off in zip(grads, offsets):
            gradient = lax.dynamic_update_slice_in_dim(gradient, g, off, axis=1)
        return (gradient, misfit)

    return shards


def solution(mesh):
    shards = make_shards(mesh.shape["paths"], mesh.shape["cols"], mesh.shape["depth"])
    return jax.shard_map(
        shards,
        mesh=mesh,
        in_specs=(
            P(("groups", "cols", "paths"), None, "depth"),
            P(("groups", "cols", "paths"), "depth"),
            P(("groups", "paths"), "depth"),
            P(("groups", "paths"), "cols"),
            P(("groups", "paths")),
            P(("groups", "paths")),
            P(("groups", "paths"), None),
            P(("groups", "paths"), None),
        ),
        out_specs=(P(("groups", "cols", "paths"), "depth"), P(("groups", "paths"), None)),
        check_vma=False,
    )
```

```python
import jax
import jax.numpy as jnp
from jax import lax
from jax.sharding import PartitionSpec as P

def shifted_copies(x, axes, count):
    copies = [x]
    for shift in range(1, count):
        perm = [(i, (i + shift) % count) for i in range(count)]
        copies.append(lax.ppermute(x, axes, perm))
    return copies


def place_by_source(copies, me, count):
    stacked = jnp.zeros((count,) + copies[0].shape, copies[0].dtype)
    for shift, piece in enumerate(copies):
        stacked = lax.dynamic_update_index_in_dim(stacked, piece, (me - shift) % count, 0)
    return stacked


def exchange_sum(x, axes, count):
    me = lax.axis_index(axes)
    return jnp.sum(place_by_source(shifted_copies(x, axes, count), me, count), axis=0)


def butterfly_sum(x, axes, count):
    step = 1
    while step < count:
        perm = [(i, i ^ step) for i in range(count)]
        x = x + lax.ppermute(x, axes, perm)
        step *= 2
    return x


def pack_rows(flat, width):
    pad = (-flat.shape[0]) % width
    return jnp.pad(flat, (0, pad)).reshape(-1, width)


def make_shards(n_paths, n_cols, n_depth):
    split = n_cols == 2

    def shards(panels, model, depth_weight, seg_len, path_start, path_end, mode_index, observed):
        own_cols, modes, depth_half = panels.shape
        path_rows, block_cols = seg_len.shape
        kept = mode_index.shape[1]
        f32, bf16 = jnp.float32, jnp.bfloat16
        p_idx = lax.axis_index("paths")
        c_idx = lax.axis_index("cols")
        d_idx = lax.axis_index("depth")

        columns = c_idx * block_cols + lax.iota(jnp.int32, block_cols)
        n_len = path_rows * own_cols
        n_mi = path_rows * kept
        if split:
            width = depth_half // 2
        else:
            width = depth_half
        if path_rows == width:
            inside_t = (columns[:, None] >= path_start[None, :]) & (columns[:, None] < path_end[None, :])
            seg_t = seg_len.T
            lengths_t = jnp.where(inside_t, seg_t, jnp.zeros_like(seg_t))
            mi_t = mode_index.T.astype(bf16)

            def small_for(target):
                cols_of = lax.dynamic_slice_in_dim(lengths_t, target * own_cols, own_cols, axis=0)
                return jnp.concatenate([cols_of, mi_t], axis=0)

            def decode(rows):
                len_b = rows[:own_cols].T.astype(f32)
                return len_b, rows[own_cols:own_cols + kept].T.astype(jnp.int32)
        else:
            inside = (columns[None, :] >= path_start[:, None]) & (columns[None, :] < path_end[:, None])
            lengths = jnp.where(inside, seg_len, jnp.zeros_like(seg_len))

            def small_for(target):
                cols_of = lax.dynamic_slice_in_dim(lengths, target * own_cols, own_cols, axis=1)
                flat = jnp.concatenate([cols_of.reshape(-1), mode_index.astype(bf16).reshape(-1)])
                return pack_rows(flat, width)

            def decode(rows):
                flat = rows.reshape(-1)
                len_b = flat[:n_len].reshape(path_rows, own_cols).astype(f32)
                return len_b, flat[n_len:n_len + n_mi].reshape(path_rows, kept).astype(jnp.int32)

        scaled = (panels.astype(f32) * model.astype(f32)[:, None, :]).astype(bf16)
        scaled = scaled.reshape(own_cols * modes, depth_half)

        if split:
            own_off = c_idx * width
            other_off = (1 - c_idx) * width
            offsets = [own_off, other_off]
            mine = lax.dynamic_slice_in_dim(depth_weight, own_off, width, axis=1)
            theirs = lax.dynamic_slice_in_dim(depth_weight, other_off, width, axis=1)
            head = [mine]
        else:
            offsets = [0]
            head = [depth_weight]
        blocks = [(head + ([theirs] if split else []), small_for(p_idx))]
        for shift in range(1, n_paths):
            target = (p_idx + shift) % n_paths
            payload = jnp.concatenate([head[0], small_for(target)], axis=0)
            perm = [(i, (i + shift) % n_paths) for i in range(n_paths)]
            got = lax.ppermute(payload, "paths", perm)
            part_rows = got[:path_rows]
            dw_parts = [part_rows]
            if split:
                dw_parts.append(lax.ppermute(part_rows, "cols", [(0, 1), (1, 0)]))
            blocks.append((dw_parts, got[path_rows:]))
        scaled_parts = [lax.dynamic_slice_in_dim(scaled, off, width, axis=1) for off in offsets]
        mode_ids = lax.iota(jnp.int32, modes)

        unpacked = []
        parts = []
        for s, (dw_parts, sm) in enumerate(blocks):
            len_own, mi_b = decode(sm)
            one_hot = (mi_b[:, :, None] == mode_ids[None, None, :]).astype(f32)
            unpacked.append((dw_parts, len_own, one_hot))
            weighted = None
            for dw_part, sc_part in zip(dw_parts, scaled_parts):
                term = lax.dot_general(
                    dw_part, sc_part, (((1,), (1,)), ((), ())), preferred_element_type=f32
                )
                weighted = term if weighted is None else weighted + term
            weighted = weighted.reshape(path_rows, own_cols, modes)
            per_mode = jnp.sum(len_own[:, :, None] * weighted, axis=1)
            part = jnp.sum(one_hot * per_mode[:, None, :], axis=2)
            parts.append(part.T)
        first = (c_idx == 0) & (d_idx == 0)
        parts[0] = parts[0] - jnp.where(first, observed.T, jnp.zeros_like(observed.T))
        canon = place_by_source(parts, p_idx, n_paths)

        local = n_cols * n_depth
        if local & (local - 1) == 0:
            misfit_all = butterfly_sum(canon, ("cols", "depth"), local)
        else:
            misfit_all = exchange_sum(canon, ("cols", "depth"), local)
        misfit_all = exchange_sum(misfit_all, "paths", n_paths)
        misfit = lax.dynamic_index_in_dim(misfit_all, p_idx, 0, keepdims=False).T
        rev = list(reversed(range(n_paths)))
        doubled = jnp.concatenate([misfit_all, misfit_all], axis=0)
        mis_rev = lax.dynamic_slice_in_dim(doubled, (p_idx + 1) % n_paths, n_paths, axis=0)
        mis_rows = jnp.swapaxes(mis_rev, 1, 2).reshape(n_paths * path_rows, kept)
        len_all = jnp.concatenate([unpacked[s][1] for s in rev], axis=0)
        hot_all = jnp.concatenate([unpacked[s][2] for s in rev], axis=0)
        resid = jnp.sum(mis_rows[:, :, None] * hot_all, axis=1)
        spread = (len_all[:, :, None] * resid[:, None, :]).astype(bf16)
        spread = spread.reshape(n_paths * path_rows, own_cols * modes)
        summed = []
        for j in range(len(offsets)):
            dw_all = jnp.concatenate([unpacked[s][0][j] for s in rev], axis=0)
            summed.append(
                lax.dot_general(
                    spread, dw_all, (((0,), (0,)), ((), ())), preferred_element_type=f32
                )
            )
        grads = []
        for acc, off in zip(summed, offsets):
            panel_part = lax.dynamic_slice_in_dim(panels, off, width, axis=2).astype(f32)
            grads.append(jnp.sum(acc.reshape(own_cols, modes, width) * panel_part, axis=1))
        gradient = jnp.zeros((own_cols, depth_half), f32)
        for g, off in zip(grads, offsets):
            gradient = lax.dynamic_update_slice_in_dim(gradient, g, off, axis=1)
        return (gradient, misfit)

    return shards


def solution(mesh):
    shards = make_shards(mesh.shape["paths"], mesh.shape["cols"], mesh.shape["depth"])
    return jax.shard_map(
        shards,
        mesh=mesh,
        in_specs=(
            P(("groups", "cols", "paths"), None, "depth"),
            P(("groups", "cols", "paths"), "depth"),
            P(("groups", "paths"), "depth"),
            P(("groups", "paths"), "cols"),
            P(("groups", "paths")),
            P(("groups", "paths")),
            P(("groups", "paths"), None),
            P(("groups", "paths"), None),
        ),
        out_specs=(P(("groups", "cols", "paths"), "depth"), P(("groups", "paths"), None)),
        check_vma=False,
    )
```

```python
import jax
import jax.numpy as jnp
from jax import lax
from jax.sharding import PartitionSpec as P

def shifted_copies(x, axes, count):
    copies = [x]
    for shift in range(1, count):
        perm = [(i, (i + shift) % count) for i in range(count)]
        copies.append(lax.ppermute(x, axes, perm))
    return copies


def place_by_source(copies, me, count):
    stacked = jnp.zeros((count,) + copies[0].shape, copies[0].dtype)
    for shift, piece in enumerate(copies):
        stacked = lax.dynamic_update_index_in_dim(stacked, piece, (me - shift) % count, 0)
    return stacked


def exchange_sum(x, axes, count):
    me = lax.axis_index(axes)
    return jnp.sum(place_by_source(shifted_copies(x, axes, count), me, count), axis=0)


def butterfly_sum(x, axes, count):
    step = 1
    while step < count:
        perm = [(i, i ^ step) for i in range(count)]
        x = x + lax.ppermute(x, axes, perm)
        step *= 2
    return x


def pack_rows(flat, width):
    pad = (-flat.shape[0]) % width
    return jnp.pad(flat, (0, pad)).reshape(-1, width)


def make_shards(n_paths, n_cols, n_depth):
    split = n_cols == 2

    def shards(panels, model, depth_weight, seg_len, path_start, path_end, mode_index, observed):
        own_cols, modes, depth_half = panels.shape
        path_rows, block_cols = seg_len.shape
        kept = mode_index.shape[1]
        f32, bf16 = jnp.float32, jnp.bfloat16
        p_idx = lax.axis_index("paths")
        c_idx = lax.axis_index("cols")
        d_idx = lax.axis_index("depth")

        columns = c_idx * block_cols + lax.iota(jnp.int32, block_cols)
        n_len = path_rows * own_cols
        n_mi = path_rows * kept
        if split:
            width = depth_half // 2
        else:
            width = depth_half
        if path_rows == width:
            inside_t = (columns[:, None] >= path_start[None, :]) & (columns[:, None] < path_end[None, :])
            seg_t = seg_len.T
            lengths_t = jnp.where(inside_t, seg_t, jnp.zeros_like(seg_t))
            mi_t = mode_index.T.astype(bf16)

            def small_for(target):
                cols_of = lax.dynamic_slice_in_dim(lengths_t, target * own_cols, own_cols, axis=0)
                return jnp.concatenate([cols_of, mi_t], axis=0)

            def decode(rows):
                len_b = rows[:own_cols].T.astype(f32)
                return len_b, rows[own_cols:own_cols + kept].T.astype(jnp.int32)
        else:
            inside = (columns[None, :] >= path_start[:, None]) & (columns[None, :] < path_end[:, None])
            lengths = jnp.where(inside, seg_len, jnp.zeros_like(seg_len))

            def small_for(target):
                cols_of = lax.dynamic_slice_in_dim(lengths, target * own_cols, own_cols, axis=1)
                flat = jnp.concatenate([cols_of.reshape(-1), mode_index.astype(bf16).reshape(-1)])
                return pack_rows(flat, width)

            def decode(rows):
                flat = rows.reshape(-1)
                len_b = flat[:n_len].reshape(path_rows, own_cols).astype(f32)
                return len_b, flat[n_len:n_len + n_mi].reshape(path_rows, kept).astype(jnp.int32)

        scaled = (panels.astype(f32) * model.astype(f32)[:, None, :]).astype(bf16)
        scaled = scaled.reshape(own_cols * modes, depth_half)

        if split:
            own_off = c_idx * width
            other_off = (1 - c_idx) * width
            offsets = [own_off, other_off]
            mine = lax.dynamic_slice_in_dim(depth_weight, own_off, width, axis=1)
            theirs = lax.dynamic_slice_in_dim(depth_weight, other_off, width, axis=1)
            head = [mine]
        else:
            offsets = [0]
            head = [depth_weight]
        blocks = [(head + ([theirs] if split else []), small_for(p_idx))]
        for shift in range(1, n_paths):
            target = (p_idx + shift) % n_paths
            payload = jnp.concatenate([head[0], small_for(target)], axis=0)
            perm = [(i, (i + shift) % n_paths) for i in range(n_paths)]
            got = lax.ppermute(payload, "paths", perm)
            part_rows = got[:path_rows]
            dw_parts = [part_rows]
            if split:
                dw_parts.append(lax.ppermute(part_rows, "cols", [(0, 1), (1, 0)]))
            blocks.append((dw_parts, got[path_rows:]))
        scaled_parts = [lax.dynamic_slice_in_dim(scaled, off, width, axis=1) for off in offsets]
        mode_ids = lax.iota(jnp.int32, modes)

        unpacked = []
        parts = []
        for s, (dw_parts, sm) in enumerate(blocks):
            len_own, mi_b = decode(sm)
            one_hot = (mi_b[:, :, None] == mode_ids[None, None, :]).astype(f32)
            unpacked.append((dw_parts, len_own, one_hot))
            weighted = None
            for dw_part, sc_part in zip(dw_parts, scaled_parts):
                term = lax.dot_general(
                    dw_part, sc_part, (((1,), (1,)), ((), ())), preferred_element_type=f32
                )
                weighted = term if weighted is None else weighted + term
            weighted = weighted.reshape(path_rows, own_cols, modes)
            per_mode = jnp.sum(len_own[:, :, None] * weighted, axis=1)
            part = jnp.sum(one_hot * per_mode[:, None, :], axis=2)
            parts.append(part.T)
        first = (c_idx == 0) & (d_idx == 0)
        parts[0] = parts[0] - jnp.where(first, observed.T, jnp.zeros_like(observed.T))
        canon = place_by_source(parts, p_idx, n_paths)

        local = n_cols * n_depth
        misfit_all = exchange_sum(canon, ("cols", "depth"), local)
        misfit_all = exchange_sum(misfit_all, "paths", n_paths)
        misfit = lax.dynamic_index_in_dim(misfit_all, p_idx, 0, keepdims=False).T
        rev = list(reversed(range(n_paths)))
        doubled = jnp.concatenate([misfit_all, misfit_all], axis=0)
        mis_rev = lax.dynamic_slice_in_dim(doubled, (p_idx + 1) % n_paths, n_paths, axis=0)
        mis_rows = jnp.swapaxes(mis_rev, 1, 2).reshape(n_paths * path_rows, kept)
        len_all = jnp.concatenate([unpacked[s][1] for s in rev], axis=0)
        hot_all = jnp.concatenate([unpacked[s][2] for s in rev], axis=0)
        resid = jnp.sum(mis_rows[:, :, None] * hot_all, axis=1)
        spread = (len_all[:, :, None] * resid[:, None, :]).astype(bf16)
        spread = spread.reshape(n_paths * path_rows, own_cols * modes)
        summed = []
        for j in range(len(offsets)):
            dw_all = jnp.concatenate([unpacked[s][0][j] for s in rev], axis=0)
            summed.append(
                lax.dot_general(
                    spread, dw_all, (((0,), (0,)), ((), ())), preferred_element_type=f32
                )
            )
        grads = []
        for acc, off in zip(summed, offsets):
            panel_part = lax.dynamic_slice_in_dim(panels, off, width, axis=2).astype(f32)
            grads.append(jnp.sum(acc.reshape(own_cols, modes, width) * panel_part, axis=1))
        gradient = jnp.zeros((own_cols, depth_half), f32)
        for g, off in zip(grads, offsets):
            gradient = lax.dynamic_update_slice_in_dim(gradient, g, off, axis=1)
        return (gradient, misfit)

    return shards


def solution(mesh):
    shards = make_shards(mesh.shape["paths"], mesh.shape["cols"], mesh.shape["depth"])
    return jax.shard_map(
        shards,
        mesh=mesh,
        in_specs=(
            P(("groups", "cols", "paths"), None, "depth"),
            P(("groups", "cols", "paths"), "depth"),
            P(("groups", "paths"), "depth"),
            P(("groups", "paths"), "cols"),
            P(("groups", "paths")),
            P(("groups", "paths")),
            P(("groups", "paths"), None),
            P(("groups", "paths"), None),
        ),
        out_specs=(P(("groups", "cols", "paths"), "depth"), P(("groups", "paths"), None)),
        check_vma=False,
    )
```

```python
import jax
import jax.numpy as jnp
from jax import lax
from jax.sharding import PartitionSpec as P

def shifted_copies(x, axes, count):
    copies = [x]
    for shift in range(1, count):
        perm = [(i, (i + shift) % count) for i in range(count)]
        copies.append(lax.ppermute(x, axes, perm))
    return copies


def place_by_source(copies, me, count):
    stacked = jnp.zeros((count,) + copies[0].shape, copies[0].dtype)
    for shift, piece in enumerate(copies):
        stacked = lax.dynamic_update_index_in_dim(stacked, piece, (me - shift) % count, 0)
    return stacked


def exchange_sum(x, axes, count):
    me = lax.axis_index(axes)
    return jnp.sum(place_by_source(shifted_copies(x, axes, count), me, count), axis=0)


def butterfly_sum(x, axes, count):
    step = 1
    while step < count:
        perm = [(i, i ^ step) for i in range(count)]
        x = x + lax.ppermute(x, axes, perm)
        step *= 2
    return x


def pack_rows(flat, width):
    pad = (-flat.shape[0]) % width
    return jnp.pad(flat, (0, pad)).reshape(-1, width)


def make_shards(n_paths, n_cols, n_depth):
    split = n_cols == 2

    def shards(panels, model, depth_weight, seg_len, path_start, path_end, mode_index, observed):
        own_cols, modes, depth_half = panels.shape
        path_rows, block_cols = seg_len.shape
        kept = mode_index.shape[1]
        f32, bf16 = jnp.float32, jnp.bfloat16
        p_idx = lax.axis_index("paths")
        c_idx = lax.axis_index("cols")
        d_idx = lax.axis_index("depth")

        columns = c_idx * block_cols + lax.iota(jnp.int32, block_cols)
        n_len = path_rows * own_cols
        n_mi = path_rows * kept
        if split:
            width = depth_half // 2
        else:
            width = depth_half
        if path_rows == width:
            inside_t = (columns[:, None] >= path_start[None, :]) & (columns[:, None] < path_end[None, :])
            seg_t = seg_len.T
            lengths_t = jnp.where(inside_t, seg_t, jnp.zeros_like(seg_t))
            mi_t = mode_index.T.astype(bf16)

            def small_for(target):
                cols_of = lax.dynamic_slice_in_dim(lengths_t, target * own_cols, own_cols, axis=0)
                return jnp.concatenate([cols_of, mi_t], axis=0)

            def decode(rows):
                len_b = rows[:own_cols].T.astype(f32)
                return len_b, rows[own_cols:own_cols + kept].T.astype(jnp.int32)
        else:
            inside = (columns[None, :] >= path_start[:, None]) & (columns[None, :] < path_end[:, None])
            lengths = jnp.where(inside, seg_len, jnp.zeros_like(seg_len))

            def small_for(target):
                cols_of = lax.dynamic_slice_in_dim(lengths, target * own_cols, own_cols, axis=1)
                flat = jnp.concatenate([cols_of.reshape(-1), mode_index.astype(bf16).reshape(-1)])
                return pack_rows(flat, width)

            def decode(rows):
                flat = rows.reshape(-1)
                len_b = flat[:n_len].reshape(path_rows, own_cols).astype(f32)
                return len_b, flat[n_len:n_len + n_mi].reshape(path_rows, kept).astype(jnp.int32)

        scaled = (panels.astype(f32) * model.astype(f32)[:, None, :]).astype(bf16)
        scaled = scaled.reshape(own_cols * modes, depth_half)

        if split:
            own_off = c_idx * width
            other_off = (1 - c_idx) * width
            offsets = [own_off, other_off]
            mine = lax.dynamic_slice_in_dim(depth_weight, own_off, width, axis=1)
            theirs = lax.dynamic_slice_in_dim(depth_weight, other_off, width, axis=1)
            head = [mine]
        else:
            offsets = [0]
            head = [depth_weight]
        blocks = [(head + ([theirs] if split else []), small_for(p_idx))]
        for shift in range(1, n_paths):
            target = (p_idx + shift) % n_paths
            payload = jnp.concatenate([head[0], small_for(target)], axis=0)
            perm = [(i, (i + shift) % n_paths) for i in range(n_paths)]
            got = lax.ppermute(payload, "paths", perm)
            part_rows = got[:path_rows]
            dw_parts = [part_rows]
            if split:
                dw_parts.append(lax.ppermute(part_rows, "cols", [(0, 1), (1, 0)]))
            blocks.append((dw_parts, got[path_rows:]))
        scaled_parts = [lax.dynamic_slice_in_dim(scaled, off, width, axis=1) for off in offsets]
        mode_ids = lax.iota(jnp.int32, modes)

        unpacked = []
        parts = []
        for s, (dw_parts, sm) in enumerate(blocks):
            len_own, mi_b = decode(sm)
            one_hot = (mi_b[:, :, None] == mode_ids[None, None, :]).astype(f32)
            unpacked.append((dw_parts, len_own, one_hot))
            weighted = None
            for dw_part, sc_part in zip(dw_parts, scaled_parts):
                term = lax.dot_general(
                    dw_part, sc_part, (((1,), (1,)), ((), ())), preferred_element_type=f32
                )
                weighted = term if weighted is None else weighted + term
            weighted = weighted.reshape(path_rows, own_cols, modes)
            per_mode = jnp.sum(len_own[:, :, None] * weighted, axis=1)
            part = jnp.sum(one_hot * per_mode[:, None, :], axis=2)
            parts.append(part.T)
        first = (c_idx == 0) & (d_idx == 0)
        parts[0] = parts[0] - jnp.where(first, observed.T, jnp.zeros_like(observed.T))
        canon = place_by_source(parts, p_idx, n_paths)

        local = n_cols * n_depth
        misfit_all = exchange_sum(canon, ("cols", "depth"), local)
        misfit_all = exchange_sum(misfit_all, "paths", n_paths)
        misfit = lax.dynamic_index_in_dim(misfit_all, p_idx, 0, keepdims=False).T
        rev = list(reversed(range(n_paths)))
        doubled = jnp.concatenate([misfit_all, misfit_all], axis=0)
        mis_rev = lax.dynamic_slice_in_dim(doubled, (p_idx + 1) % n_paths, n_paths, axis=0)
        mis_rows = jnp.swapaxes(mis_rev, 1, 2).reshape(n_paths * path_rows, kept)
        len_all = jnp.concatenate([unpacked[s][1] for s in rev], axis=0)
        hot_all = jnp.concatenate([unpacked[s][2] for s in rev], axis=0)
        resid = jnp.sum(mis_rows[:, :, None] * hot_all, axis=1)
        spread = (len_all[:, :, None] * resid[:, None, :]).astype(bf16)
        spread = spread.reshape(n_paths * path_rows, own_cols * modes)
        full_blocks = []
        for s in rev:
            full = unpacked[s][0][0] if len(offsets) == 1 else jnp.zeros((path_rows, depth_half), bf16)
            if len(offsets) > 1:
                for dw_part, off in zip(unpacked[s][0], offsets):
                    full = lax.dynamic_update_slice_in_dim(full, dw_part, off, axis=1)
            full_blocks.append(full)
        dw_all = jnp.concatenate(full_blocks, axis=0)
        summed = lax.dot_general(
            spread, dw_all, (((0,), (0,)), ((), ())), preferred_element_type=f32
        ).reshape(own_cols, modes, depth_half)
        gradient = jnp.sum(summed * panels.astype(f32), axis=1)
        return (gradient, misfit)

    return shards


def solution(mesh):
    shards = make_shards(mesh.shape["paths"], mesh.shape["cols"], mesh.shape["depth"])
    return jax.shard_map(
        shards,
        mesh=mesh,
        in_specs=(
            P(("groups", "cols", "paths"), None, "depth"),
            P(("groups", "cols", "paths"), "depth"),
            P(("groups", "paths"), "depth"),
            P(("groups", "paths"), "cols"),
            P(("groups", "paths")),
            P(("groups", "paths")),
            P(("groups", "paths"), None),
            P(("groups", "paths"), None),
        ),
        out_specs=(P(("groups", "cols", "paths"), "depth"), P(("groups", "paths"), None)),
        check_vma=False,
    )
```

```python
import jax
import jax.numpy as jnp
from jax import lax
from jax.sharding import PartitionSpec as P

def shifted_copies(x, axes, count):
    copies = [x]
    for shift in range(1, count):
        perm = [(i, (i + shift) % count) for i in range(count)]
        copies.append(lax.ppermute(x, axes, perm))
    return copies


def place_by_source(copies, me, count):
    stacked = jnp.zeros((count,) + copies[0].shape, copies[0].dtype)
    for shift, piece in enumerate(copies):
        stacked = lax.dynamic_update_index_in_dim(stacked, piece, (me - shift) % count, 0)
    return stacked


def exchange_sum(x, axes, count):
    me = lax.axis_index(axes)
    return jnp.sum(place_by_source(shifted_copies(x, axes, count), me, count), axis=0)


def butterfly_sum(x, axes, count):
    step = 1
    while step < count:
        perm = [(i, i ^ step) for i in range(count)]
        x = x + lax.ppermute(x, axes, perm)
        step *= 2
    return x


def pack_rows(flat, width):
    pad = (-flat.shape[0]) % width
    return jnp.pad(flat, (0, pad)).reshape(-1, width)


def make_shards(n_paths, n_cols, n_depth):
    split = n_cols == 2

    def shards(panels, model, depth_weight, seg_len, path_start, path_end, mode_index, observed):
        own_cols, modes, depth_half = panels.shape
        path_rows, block_cols = seg_len.shape
        kept = mode_index.shape[1]
        f32, bf16 = jnp.float32, jnp.bfloat16
        p_idx = lax.axis_index("paths")
        c_idx = lax.axis_index("cols")
        d_idx = lax.axis_index("depth")

        columns = c_idx * block_cols + lax.iota(jnp.int32, block_cols)
        n_len = path_rows * own_cols
        n_mi = path_rows * kept
        if split:
            width = depth_half // 2
        else:
            width = depth_half
        if path_rows == width:
            inside_t = (columns[:, None] >= path_start[None, :]) & (columns[:, None] < path_end[None, :])
            seg_t = seg_len.T
            lengths_t = jnp.where(inside_t, seg_t, jnp.zeros_like(seg_t))
            mi_t = mode_index.T.astype(bf16)

            def small_for(target):
                cols_of = lax.dynamic_slice_in_dim(lengths_t, target * own_cols, own_cols, axis=0)
                return jnp.concatenate([cols_of, mi_t], axis=0)

            def decode(rows):
                len_b = rows[:own_cols].T.astype(f32)
                return len_b, rows[own_cols:own_cols + kept].T.astype(jnp.int32)
        else:
            inside = (columns[None, :] >= path_start[:, None]) & (columns[None, :] < path_end[:, None])
            lengths = jnp.where(inside, seg_len, jnp.zeros_like(seg_len))

            def small_for(target):
                cols_of = lax.dynamic_slice_in_dim(lengths, target * own_cols, own_cols, axis=1)
                flat = jnp.concatenate([cols_of.reshape(-1), mode_index.astype(bf16).reshape(-1)])
                return pack_rows(flat, width)

            def decode(rows):
                flat = rows.reshape(-1)
                len_b = flat[:n_len].reshape(path_rows, own_cols).astype(f32)
                return len_b, flat[n_len:n_len + n_mi].reshape(path_rows, kept).astype(jnp.int32)

        scaled = (panels.astype(f32) * model.astype(f32)[:, None, :]).astype(bf16)
        scaled = scaled.reshape(own_cols * modes, depth_half)

        if split:
            own_off = c_idx * width
            other_off = (1 - c_idx) * width
            offsets = [own_off, other_off]
            mine = lax.dynamic_slice_in_dim(depth_weight, own_off, width, axis=1)
            theirs = lax.dynamic_slice_in_dim(depth_weight, other_off, width, axis=1)
            head = [mine]
        else:
            offsets = [0]
            head = [depth_weight]
        blocks = [(head + ([theirs] if split else []), small_for(p_idx))]
        for shift in range(1, n_paths):
            target = (p_idx + shift) % n_paths
            payload = jnp.concatenate([head[0], small_for(target)], axis=0)
            perm = [(i, (i + shift) % n_paths) for i in range(n_paths)]
            got = lax.ppermute(payload, "paths", perm)
            part_rows = got[:path_rows]
            dw_parts = [part_rows]
            if split:
                dw_parts.append(lax.ppermute(part_rows, "cols", [(0, 1), (1, 0)]))
            blocks.append((dw_parts, got[path_rows:]))
        scaled_parts = [lax.dynamic_slice_in_dim(scaled, off, width, axis=1) for off in offsets]
        mode_ids = lax.iota(jnp.int32, modes)

        unpacked = []
        parts = []
        for s, (dw_parts, sm) in enumerate(blocks):
            len_own, mi_b = decode(sm)
            one_hot = (mi_b[:, :, None] == mode_ids[None, None, :]).astype(f32)
            unpacked.append((dw_parts, len_own, one_hot))
            weighted = None
            for dw_part, sc_part in zip(dw_parts, scaled_parts):
                term = lax.dot_general(
                    dw_part, sc_part, (((1,), (1,)), ((), ())), preferred_element_type=f32
                )
                weighted = term if weighted is None else weighted + term
            weighted = weighted.reshape(path_rows, own_cols, modes)
            per_mode = jnp.sum(len_own[:, :, None] * weighted, axis=1)
            part = jnp.sum(one_hot * per_mode[:, None, :], axis=2)
            parts.append(part.T)
        first = (c_idx == 0) & (d_idx == 0)
        parts[0] = parts[0] - jnp.where(first, observed.T, jnp.zeros_like(observed.T))
        canon = place_by_source(parts, p_idx, n_paths)

        local = n_cols * n_depth
        misfit_all = exchange_sum(canon, ("cols", "depth"), local)
        misfit_all = exchange_sum(misfit_all, "paths", n_paths)
        rev = list(reversed(range(n_paths)))
        doubled = jnp.concatenate([misfit_all, misfit_all], axis=0)
        mis_rev = lax.dynamic_slice_in_dim(doubled, (p_idx + 1) % n_paths, n_paths, axis=0)
        mis_rows = jnp.swapaxes(mis_rev, 1, 2).reshape(n_paths * path_rows, kept)
        misfit = mis_rev[n_paths - 1].T
        len_all = jnp.concatenate([unpacked[s][1] for s in rev], axis=0)
        hot_all = jnp.concatenate([unpacked[s][2] for s in rev], axis=0)
        resid = jnp.sum(mis_rows[:, :, None] * hot_all, axis=1)
        spread = (len_all[:, :, None] * resid[:, None, :]).astype(bf16)
        spread = spread.reshape(n_paths * path_rows, own_cols * modes)
        summed = []
        for j in range(len(offsets)):
            dw_all = jnp.concatenate([unpacked[s][0][j] for s in rev], axis=0)
            summed.append(
                lax.dot_general(
                    spread, dw_all, (((0,), (0,)), ((), ())), preferred_element_type=f32
                )
            )
        grads = []
        for acc, off in zip(summed, offsets):
            panel_part = lax.dynamic_slice_in_dim(panels, off, width, axis=2).astype(f32)
            grads.append(jnp.sum(acc.reshape(own_cols, modes, width) * panel_part, axis=1))
        gradient = jnp.zeros((own_cols, depth_half), f32)
        for g, off in zip(grads, offsets):
            gradient = lax.dynamic_update_slice_in_dim(gradient, g, off, axis=1)
        return (gradient, misfit)

    return shards


def solution(mesh):
    shards = make_shards(mesh.shape["paths"], mesh.shape["cols"], mesh.shape["depth"])
    return jax.shard_map(
        shards,
        mesh=mesh,
        in_specs=(
            P(("groups", "cols", "paths"), None, "depth"),
            P(("groups", "cols", "paths"), "depth"),
            P(("groups", "paths"), "depth"),
            P(("groups", "paths"), "cols"),
            P(("groups", "paths")),
            P(("groups", "paths")),
            P(("groups", "paths"), None),
            P(("groups", "paths"), None),
        ),
        out_specs=(P(("groups", "cols", "paths"), "depth"), P(("groups", "paths"), None)),
        check_vma=False,
    )
```

```python
import jax
import jax.numpy as jnp
from jax import lax
from jax.sharding import PartitionSpec as P

def shifted_copies(x, axes, count):
    copies = [x]
    for shift in range(1, count):
        perm = [(i, (i + shift) % count) for i in range(count)]
        copies.append(lax.ppermute(x, axes, perm))
    return copies


def place_by_source(copies, me, count):
    stacked = jnp.zeros((count,) + copies[0].shape, copies[0].dtype)
    for shift, piece in enumerate(copies):
        stacked = lax.dynamic_update_index_in_dim(stacked, piece, (me - shift) % count, 0)
    return stacked


def exchange_sum(x, axes, count):
    me = lax.axis_index(axes)
    return jnp.sum(place_by_source(shifted_copies(x, axes, count), me, count), axis=0)


def butterfly_sum(x, axes, count):
    step = 1
    while step < count:
        perm = [(i, i ^ step) for i in range(count)]
        x = x + lax.ppermute(x, axes, perm)
        step *= 2
    return x


def pack_rows(flat, width):
    pad = (-flat.shape[0]) % width
    return jnp.pad(flat, (0, pad)).reshape(-1, width)


def make_shards(n_paths, n_cols, n_depth):
    split = n_cols == 2

    def shards(panels, model, depth_weight, seg_len, path_start, path_end, mode_index, observed):
        own_cols, modes, depth_half = panels.shape
        path_rows, block_cols = seg_len.shape
        kept = mode_index.shape[1]
        f32, bf16 = jnp.float32, jnp.bfloat16
        p_idx = lax.axis_index("paths")
        c_idx = lax.axis_index("cols")
        d_idx = lax.axis_index("depth")

        columns = c_idx * block_cols + lax.iota(jnp.int32, block_cols)
        n_len = path_rows * own_cols
        n_mi = path_rows * kept
        if split:
            width = depth_half // 2
        else:
            width = depth_half
        if path_rows == width:
            inside_t = (columns[:, None] >= path_start[None, :]) & (columns[:, None] < path_end[None, :])
            seg_t = seg_len.T
            lengths_t = jnp.where(inside_t, seg_t, jnp.zeros_like(seg_t))
            mi_t = mode_index.T.astype(bf16)

            def small_for(target):
                cols_of = lax.dynamic_slice_in_dim(lengths_t, target * own_cols, own_cols, axis=0)
                return jnp.concatenate([cols_of, mi_t], axis=0)

            def decode(rows):
                len_b = rows[:own_cols].T.astype(f32)
                return len_b, rows[own_cols:own_cols + kept].T.astype(jnp.int32)
        else:
            inside = (columns[None, :] >= path_start[:, None]) & (columns[None, :] < path_end[:, None])
            lengths = jnp.where(inside, seg_len, jnp.zeros_like(seg_len))

            def small_for(target):
                cols_of = lax.dynamic_slice_in_dim(lengths, target * own_cols, own_cols, axis=1)
                flat = jnp.concatenate([cols_of.reshape(-1), mode_index.astype(bf16).reshape(-1)])
                return pack_rows(flat, width)

            def decode(rows):
                flat = rows.reshape(-1)
                len_b = flat[:n_len].reshape(path_rows, own_cols).astype(f32)
                return len_b, flat[n_len:n_len + n_mi].reshape(path_rows, kept).astype(jnp.int32)

        scaled = (panels.astype(f32) * model.astype(f32)[:, None, :]).astype(bf16)
        scaled = scaled.reshape(own_cols * modes, depth_half)

        if split:
            own_off = c_idx * width
            other_off = (1 - c_idx) * width
            offsets = [own_off, other_off]
            mine = lax.dynamic_slice_in_dim(depth_weight, own_off, width, axis=1)
            theirs = lax.dynamic_slice_in_dim(depth_weight, other_off, width, axis=1)
            head = [mine]
        else:
            offsets = [0]
            head = [depth_weight]
        blocks = [(head + ([theirs] if split else []), small_for(p_idx))]
        for shift in range(1, n_paths):
            target = (p_idx + shift) % n_paths
            payload = jnp.concatenate([head[0], small_for(target)], axis=0)
            perm = [(i, (i + shift) % n_paths) for i in range(n_paths)]
            got = lax.ppermute(payload, "paths", perm)
            part_rows = got[:path_rows]
            dw_parts = [part_rows]
            if split:
                dw_parts.append(lax.ppermute(part_rows, "cols", [(0, 1), (1, 0)]))
            blocks.append((dw_parts, got[path_rows:]))
        scaled_parts = [lax.dynamic_slice_in_dim(scaled, off, width, axis=1) for off in offsets]
        mode_ids = lax.iota(jnp.int32, modes)

        unpacked = []
        parts = []
        for s, (dw_parts, sm) in enumerate(blocks):
            len_own, mi_b = decode(sm)
            one_hot = (mi_b[:, :, None] == mode_ids[None, None, :]).astype(f32)
            unpacked.append((dw_parts, len_own, one_hot))
            weighted = None
            for dw_part, sc_part in zip(dw_parts, scaled_parts):
                term = lax.dot_general(
                    dw_part, sc_part, (((1,), (1,)), ((), ())), preferred_element_type=f32
                )
                weighted = term if weighted is None else weighted + term
            weighted = weighted.reshape(path_rows, own_cols, modes)
            per_mode = jnp.sum(len_own[:, :, None] * weighted, axis=1)
            part = jnp.sum(one_hot * per_mode[:, None, :], axis=2)
            parts.append(part.T)
        first = (c_idx == 0) & (d_idx == 0)
        parts[0] = parts[0] - jnp.where(first, observed.T, jnp.zeros_like(observed.T))
        canon = place_by_source(parts, p_idx, n_paths)

        local = n_cols * n_depth
        misfit_all = exchange_sum(canon, ("cols", "depth"), local)
        if n_paths & (n_paths - 1) == 0:
            misfit_all = butterfly_sum(misfit_all, "paths", n_paths)
        else:
            misfit_all = exchange_sum(misfit_all, "paths", n_paths)
        misfit = lax.dynamic_index_in_dim(misfit_all, p_idx, 0, keepdims=False).T
        rev = list(reversed(range(n_paths)))
        doubled = jnp.concatenate([misfit_all, misfit_all], axis=0)
        mis_rev = lax.dynamic_slice_in_dim(doubled, (p_idx + 1) % n_paths, n_paths, axis=0)
        mis_rows = jnp.swapaxes(mis_rev, 1, 2).reshape(n_paths * path_rows, kept)
        len_all = jnp.concatenate([unpacked[s][1] for s in rev], axis=0)
        hot_all = jnp.concatenate([unpacked[s][2] for s in rev], axis=0)
        resid = jnp.sum(mis_rows[:, :, None] * hot_all, axis=1)
        spread = (len_all[:, :, None] * resid[:, None, :]).astype(bf16)
        spread = spread.reshape(n_paths * path_rows, own_cols * modes)
        summed = []
        for j in range(len(offsets)):
            dw_all = jnp.concatenate([unpacked[s][0][j] for s in rev], axis=0)
            summed.append(
                lax.dot_general(
                    spread, dw_all, (((0,), (0,)), ((), ())), preferred_element_type=f32
                )
            )
        grads = []
        for acc, off in zip(summed, offsets):
            panel_part = lax.dynamic_slice_in_dim(panels, off, width, axis=2).astype(f32)
            grads.append(jnp.sum(acc.reshape(own_cols, modes, width) * panel_part, axis=1))
        gradient = jnp.zeros((own_cols, depth_half), f32)
        for g, off in zip(grads, offsets):
            gradient = lax.dynamic_update_slice_in_dim(gradient, g, off, axis=1)
        return (gradient, misfit)

    return shards


def solution(mesh):
    shards = make_shards(mesh.shape["paths"], mesh.shape["cols"], mesh.shape["depth"])
    return jax.shard_map(
        shards,
        mesh=mesh,
        in_specs=(
            P(("groups", "cols", "paths"), None, "depth"),
            P(("groups", "cols", "paths"), "depth"),
            P(("groups", "paths"), "depth"),
            P(("groups", "paths"), "cols"),
            P(("groups", "paths")),
            P(("groups", "paths")),
            P(("groups", "paths"), None),
            P(("groups", "paths"), None),
        ),
        out_specs=(P(("groups", "cols", "paths"), "depth"), P(("groups", "paths"), None)),
        check_vma=False,
    )
```

```python
import jax
import jax.numpy as jnp
from jax import lax
from jax.sharding import PartitionSpec as P

def shifted_copies(x, axes, count):
    copies = [x]
    for shift in range(1, count):
        perm = [(i, (i + shift) % count) for i in range(count)]
        copies.append(lax.ppermute(x, axes, perm))
    return copies


def place_by_source(copies, me, count):
    stacked = jnp.zeros((count,) + copies[0].shape, copies[0].dtype)
    for shift, piece in enumerate(copies):
        stacked = lax.dynamic_update_index_in_dim(stacked, piece, (me - shift) % count, 0)
    return stacked


def exchange_sum(x, axes, count):
    me = lax.axis_index(axes)
    return jnp.sum(place_by_source(shifted_copies(x, axes, count), me, count), axis=0)


def butterfly_sum(x, axes, count):
    step = 1
    while step < count:
        perm = [(i, i ^ step) for i in range(count)]
        x = x + lax.ppermute(x, axes, perm)
        step *= 2
    return x


def pack_rows(flat, width):
    pad = (-flat.shape[0]) % width
    return jnp.pad(flat, (0, pad)).reshape(-1, width)


def make_shards(n_paths, n_cols, n_depth):
    split = n_cols == 2

    def shards(panels, model, depth_weight, seg_len, path_start, path_end, mode_index, observed):
        own_cols, modes, depth_half = panels.shape
        path_rows, block_cols = seg_len.shape
        kept = mode_index.shape[1]
        f32, bf16 = jnp.float32, jnp.bfloat16
        p_idx = lax.axis_index("paths")
        c_idx = lax.axis_index("cols")
        d_idx = lax.axis_index("depth")

        columns = c_idx * block_cols + lax.iota(jnp.int32, block_cols)
        n_len = path_rows * own_cols
        n_mi = path_rows * kept
        if split:
            width = depth_half // 2
        else:
            width = depth_half
        if path_rows == width:
            inside_t = (columns[:, None] >= path_start[None, :]) & (columns[:, None] < path_end[None, :])
            seg_t = seg_len.T
            lengths_t = jnp.where(inside_t, seg_t, jnp.zeros_like(seg_t))
            mi_t = mode_index.T.astype(bf16)

            def small_for(target):
                cols_of = lax.dynamic_slice_in_dim(lengths_t, target * own_cols, own_cols, axis=0)
                return jnp.concatenate([cols_of, mi_t], axis=0)

            def decode(rows):
                len_b = rows[:own_cols].T.astype(f32)
                return len_b, rows[own_cols:own_cols + kept].T.astype(jnp.int32)
        else:
            inside = (columns[None, :] >= path_start[:, None]) & (columns[None, :] < path_end[:, None])
            lengths = jnp.where(inside, seg_len, jnp.zeros_like(seg_len))

            def small_for(target):
                cols_of = lax.dynamic_slice_in_dim(lengths, target * own_cols, own_cols, axis=1)
                flat = jnp.concatenate([cols_of.reshape(-1), mode_index.astype(bf16).reshape(-1)])
                return pack_rows(flat, width)

            def decode(rows):
                flat = rows.reshape(-1)
                len_b = flat[:n_len].reshape(path_rows, own_cols).astype(f32)
                return len_b, flat[n_len:n_len + n_mi].reshape(path_rows, kept).astype(jnp.int32)

        scaled = (panels.astype(f32) * model.astype(f32)[:, None, :]).astype(bf16)
        scaled = scaled.reshape(own_cols * modes, depth_half)

        if split:
            own_off = c_idx * width
            other_off = (1 - c_idx) * width
            offsets = [own_off, other_off]
            mine = lax.dynamic_slice_in_dim(depth_weight, own_off, width, axis=1)
            theirs = lax.dynamic_slice_in_dim(depth_weight, other_off, width, axis=1)
            head = [mine]
        else:
            offsets = [0]
            head = [depth_weight]
        blocks = [(head + ([theirs] if split else []), small_for(p_idx))]
        for shift in range(1, n_paths):
            target = (p_idx + shift) % n_paths
            payload = jnp.concatenate([head[0], small_for(target)], axis=0)
            perm = [(i, (i + shift) % n_paths) for i in range(n_paths)]
            got = lax.ppermute(payload, "paths", perm)
            part_rows = got[:path_rows]
            dw_parts = [part_rows]
            if split:
                dw_parts.append(lax.ppermute(part_rows, "cols", [(0, 1), (1, 0)]))
            blocks.append((dw_parts, got[path_rows:]))
        scaled_parts = [lax.dynamic_slice_in_dim(scaled, off, width, axis=1) for off in offsets]
        mode_ids = lax.iota(jnp.int32, modes)

        unpacked = []
        parts = []
        for s, (dw_parts, sm) in enumerate(blocks):
            len_own, mi_b = decode(sm)
            one_hot = (mi_b[:, :, None] == mode_ids[None, None, :]).astype(f32)
            unpacked.append((dw_parts, len_own, one_hot))
            part = None
            for dw_part, sc_part in zip(dw_parts, scaled_parts):
                weighted = lax.dot_general(
                    dw_part, sc_part, (((1,), (1,)), ((), ())), preferred_element_type=f32
                ).reshape(path_rows, own_cols, modes)
                per_mode = jnp.sum(len_own[:, :, None] * weighted, axis=1)
                term = jnp.sum(one_hot * per_mode[:, None, :], axis=2)
                part = term if part is None else part + term
            parts.append(part.T)
        first = (c_idx == 0) & (d_idx == 0)
        parts[0] = parts[0] - jnp.where(first, observed.T, jnp.zeros_like(observed.T))
        canon = place_by_source(parts, p_idx, n_paths)

        local = n_cols * n_depth
        misfit_all = exchange_sum(canon, ("cols", "depth"), local)
        misfit_all = exchange_sum(misfit_all, "paths", n_paths)
        misfit = lax.dynamic_index_in_dim(misfit_all, p_idx, 0, keepdims=False).T
        rev = list(reversed(range(n_paths)))
        doubled = jnp.concatenate([misfit_all, misfit_all], axis=0)
        mis_rev = lax.dynamic_slice_in_dim(doubled, (p_idx + 1) % n_paths, n_paths, axis=0)
        mis_rows = jnp.swapaxes(mis_rev, 1, 2).reshape(n_paths * path_rows, kept)
        len_all = jnp.concatenate([unpacked[s][1] for s in rev], axis=0)
        hot_all = jnp.concatenate([unpacked[s][2] for s in rev], axis=0)
        resid = jnp.sum(mis_rows[:, :, None] * hot_all, axis=1)
        spread = (len_all[:, :, None] * resid[:, None, :]).astype(bf16)
        spread = spread.reshape(n_paths * path_rows, own_cols * modes)
        summed = []
        for j in range(len(offsets)):
            dw_all = jnp.concatenate([unpacked[s][0][j] for s in rev], axis=0)
            summed.append(
                lax.dot_general(
                    spread, dw_all, (((0,), (0,)), ((), ())), preferred_element_type=f32
                )
            )
        grads = []
        for acc, off in zip(summed, offsets):
            panel_part = lax.dynamic_slice_in_dim(panels, off, width, axis=2).astype(f32)
            grads.append(jnp.sum(acc.reshape(own_cols, modes, width) * panel_part, axis=1))
        gradient = jnp.zeros((own_cols, depth_half), f32)
        for g, off in zip(grads, offsets):
            gradient = lax.dynamic_update_slice_in_dim(gradient, g, off, axis=1)
        return (gradient, misfit)

    return shards


def solution(mesh):
    shards = make_shards(mesh.shape["paths"], mesh.shape["cols"], mesh.shape["depth"])
    return jax.shard_map(
        shards,
        mesh=mesh,
        in_specs=(
            P(("groups", "cols", "paths"), None, "depth"),
            P(("groups", "cols", "paths"), "depth"),
            P(("groups", "paths"), "depth"),
            P(("groups", "paths"), "cols"),
            P(("groups", "paths")),
            P(("groups", "paths")),
            P(("groups", "paths"), None),
            P(("groups", "paths"), None),
        ),
        out_specs=(P(("groups", "cols", "paths"), "depth"), P(("groups", "paths"), None)),
        check_vma=False,
    )
```

```python
import jax
import jax.numpy as jnp
from jax import lax
from jax.sharding import PartitionSpec as P

def shifted_copies(x, axes, count):
    copies = [x]
    for shift in range(1, count):
        perm = [(i, (i + shift) % count) for i in range(count)]
        copies.append(lax.ppermute(x, axes, perm))
    return copies


def place_by_source(copies, me, count):
    stacked = jnp.zeros((count,) + copies[0].shape, copies[0].dtype)
    for shift, piece in enumerate(copies):
        stacked = lax.dynamic_update_index_in_dim(stacked, piece, (me - shift) % count, 0)
    return stacked


def exchange_sum(x, axes, count):
    me = lax.axis_index(axes)
    return jnp.sum(place_by_source(shifted_copies(x, axes, count), me, count), axis=0)


def butterfly_sum(x, axes, count):
    step = 1
    while step < count:
        perm = [(i, i ^ step) for i in range(count)]
        x = x + lax.ppermute(x, axes, perm)
        step *= 2
    return x


def pack_rows(flat, width):
    pad = (-flat.shape[0]) % width
    return jnp.pad(flat, (0, pad)).reshape(-1, width)


def make_shards(n_paths, n_cols, n_depth):
    split = n_cols == 2

    def shards(panels, model, depth_weight, seg_len, path_start, path_end, mode_index, observed):
        own_cols, modes, depth_half = panels.shape
        path_rows, block_cols = seg_len.shape
        kept = mode_index.shape[1]
        f32, bf16 = jnp.float32, jnp.bfloat16
        p_idx = lax.axis_index("paths")
        c_idx = lax.axis_index("cols")
        d_idx = lax.axis_index("depth")

        columns = c_idx * block_cols + lax.iota(jnp.int32, block_cols)
        n_len = path_rows * own_cols
        n_mi = path_rows * kept
        if split:
            width = depth_half // 2
        else:
            width = depth_half
        if path_rows == width:
            inside_t = (columns[:, None] >= path_start[None, :]) & (columns[:, None] < path_end[None, :])
            seg_t = seg_len.T
            lengths_t = jnp.where(inside_t, seg_t, jnp.zeros_like(seg_t))
            mi_t = mode_index.T.astype(bf16)

            def small_for(target):
                cols_of = lax.dynamic_slice_in_dim(lengths_t, target * own_cols, own_cols, axis=0)
                return jnp.concatenate([cols_of, mi_t], axis=0)

            def decode(rows):
                len_b = rows[:own_cols].T.astype(f32)
                return len_b, rows[own_cols:own_cols + kept].T.astype(jnp.int32)
        else:
            inside = (columns[None, :] >= path_start[:, None]) & (columns[None, :] < path_end[:, None])
            lengths = jnp.where(inside, seg_len, jnp.zeros_like(seg_len))

            def small_for(target):
                cols_of = lax.dynamic_slice_in_dim(lengths, target * own_cols, own_cols, axis=1)
                flat = jnp.concatenate([cols_of.reshape(-1), mode_index.astype(bf16).reshape(-1)])
                return pack_rows(flat, width)

            def decode(rows):
                flat = rows.reshape(-1)
                len_b = flat[:n_len].reshape(path_rows, own_cols).astype(f32)
                return len_b, flat[n_len:n_len + n_mi].reshape(path_rows, kept).astype(jnp.int32)

        scaled = (panels.astype(f32) * model.astype(f32)[:, None, :]).astype(bf16)
        scaled = scaled.reshape(own_cols * modes, depth_half)

        if split:
            own_off = c_idx * width
            other_off = (1 - c_idx) * width
            offsets = [own_off, other_off]
            mine = lax.dynamic_slice_in_dim(depth_weight, own_off, width, axis=1)
            head = [mine]
        else:
            offsets = [0]
            head = [depth_weight]
        blocks = [(list(head), small_for(p_idx))]
        for shift in range(1, n_paths):
            target = (p_idx + shift) % n_paths
            payload = jnp.concatenate([head[0], small_for(target)], axis=0)
            perm = [(i, (i + shift) % n_paths) for i in range(n_paths)]
            got = lax.ppermute(payload, "paths", perm)
            part_rows = got[:path_rows]
            dw_parts = [part_rows]
            if split:
                dw_parts.append(lax.ppermute(part_rows, "cols", [(0, 1), (1, 0)]))
            blocks.append((dw_parts, got[path_rows:]))
        if split:
            late_dw = depth_weight
            if len(blocks) > 1:
                late_dw, _ = lax.optimization_barrier((depth_weight, blocks[1][0][0]))
            blocks[0][0].append(lax.dynamic_slice_in_dim(late_dw, other_off, width, axis=1))
        scaled_parts = [lax.dynamic_slice_in_dim(scaled, off, width, axis=1) for off in offsets]
        mode_ids = lax.iota(jnp.int32, modes)

        unpacked = []
        parts = []
        for s, (dw_parts, sm) in enumerate(blocks):
            len_own, mi_b = decode(sm)
            one_hot = (mi_b[:, :, None] == mode_ids[None, None, :]).astype(f32)
            unpacked.append((dw_parts, len_own, one_hot))
            part = None
            for dw_part, sc_part in zip(dw_parts, scaled_parts):
                weighted = lax.dot_general(
                    dw_part, sc_part, (((1,), (1,)), ((), ())), preferred_element_type=f32
                ).reshape(path_rows, own_cols, modes)
                per_mode = jnp.sum(len_own[:, :, None] * weighted, axis=1)
                term = jnp.sum(one_hot * per_mode[:, None, :], axis=2)
                part = term if part is None else part + term
            parts.append(part.T)
        first = (c_idx == 0) & (d_idx == 0)
        parts[0] = parts[0] - jnp.where(first, observed.T, jnp.zeros_like(observed.T))
        canon = place_by_source(parts, p_idx, n_paths)

        local = n_cols * n_depth
        misfit_all = exchange_sum(canon, ("cols", "depth"), local)
        misfit_all = exchange_sum(misfit_all, "paths", n_paths)
        misfit = lax.dynamic_index_in_dim(misfit_all, p_idx, 0, keepdims=False).T
        rev = list(reversed(range(n_paths)))
        doubled = jnp.concatenate([misfit_all, misfit_all], axis=0)
        mis_rev = lax.dynamic_slice_in_dim(doubled, (p_idx + 1) % n_paths, n_paths, axis=0)
        mis_rows = jnp.swapaxes(mis_rev, 1, 2).reshape(n_paths * path_rows, kept)
        len_all = jnp.concatenate([unpacked[s][1] for s in rev], axis=0)
        hot_all = jnp.concatenate([unpacked[s][2] for s in rev], axis=0)
        resid = jnp.sum(mis_rows[:, :, None] * hot_all, axis=1)
        spread = (len_all[:, :, None] * resid[:, None, :]).astype(bf16)
        spread = spread.reshape(n_paths * path_rows, own_cols * modes)
        summed = []
        for j in range(len(offsets)):
            dw_all = jnp.concatenate([unpacked[s][0][j] for s in rev], axis=0)
            summed.append(
                lax.dot_general(
                    spread, dw_all, (((0,), (0,)), ((), ())), preferred_element_type=f32
                )
            )
        grads = []
        for acc, off in zip(summed, offsets):
            panel_part = lax.dynamic_slice_in_dim(panels, off, width, axis=2).astype(f32)
            grads.append(jnp.sum(acc.reshape(own_cols, modes, width) * panel_part, axis=1))
        gradient = jnp.zeros((own_cols, depth_half), f32)
        for g, off in zip(grads, offsets):
            gradient = lax.dynamic_update_slice_in_dim(gradient, g, off, axis=1)
        return (gradient, misfit)

    return shards


def solution(mesh):
    shards = make_shards(mesh.shape["paths"], mesh.shape["cols"], mesh.shape["depth"])
    return jax.shard_map(
        shards,
        mesh=mesh,
        in_specs=(
            P(("groups", "cols", "paths"), None, "depth"),
            P(("groups", "cols", "paths"), "depth"),
            P(("groups", "paths"), "depth"),
            P(("groups", "paths"), "cols"),
            P(("groups", "paths")),
            P(("groups", "paths")),
            P(("groups", "paths"), None),
            P(("groups", "paths"), None),
        ),
        out_specs=(P(("groups", "cols", "paths"), "depth"), P(("groups", "paths"), None)),
        check_vma=False,
    )
```

```python
import jax
import jax.numpy as jnp
from jax import lax
from jax.sharding import PartitionSpec as P

def shifted_copies(x, axes, count):
    copies = [x]
    for shift in range(1, count):
        perm = [(i, (i + shift) % count) for i in range(count)]
        copies.append(lax.ppermute(x, axes, perm))
    return copies


def place_by_source(copies, me, count):
    stacked = jnp.zeros((count,) + copies[0].shape, copies[0].dtype)
    for shift, piece in enumerate(copies):
        stacked = lax.dynamic_update_index_in_dim(stacked, piece, (me - shift) % count, 0)
    return stacked


def exchange_sum(x, axes, count):
    me = lax.axis_index(axes)
    return jnp.sum(place_by_source(shifted_copies(x, axes, count), me, count), axis=0)


def butterfly_sum(x, axes, count):
    step = 1
    while step < count:
        perm = [(i, i ^ step) for i in range(count)]
        x = x + lax.ppermute(x, axes, perm)
        step *= 2
    return x


def pack_rows(flat, width):
    pad = (-flat.shape[0]) % width
    return jnp.pad(flat, (0, pad)).reshape(-1, width)


def make_shards(n_paths, n_cols, n_depth):
    split = n_cols == 2

    def shards(panels, model, depth_weight, seg_len, path_start, path_end, mode_index, observed):
        own_cols, modes, depth_half = panels.shape
        path_rows, block_cols = seg_len.shape
        kept = mode_index.shape[1]
        f32, bf16 = jnp.float32, jnp.bfloat16
        p_idx = lax.axis_index("paths")
        c_idx = lax.axis_index("cols")
        d_idx = lax.axis_index("depth")

        columns = c_idx * block_cols + lax.iota(jnp.int32, block_cols)
        n_len = path_rows * own_cols
        n_mi = path_rows * kept
        if split:
            width = depth_half // 2
        else:
            width = depth_half
        if path_rows == width:
            inside_t = (columns[:, None] >= path_start[None, :]) & (columns[:, None] < path_end[None, :])
            seg_t = seg_len.T
            lengths_t = jnp.where(inside_t, seg_t, jnp.zeros_like(seg_t))
            mi_t = mode_index.T.astype(bf16)

            def small_for(target):
                cols_of = lax.dynamic_slice_in_dim(lengths_t, target * own_cols, own_cols, axis=0)
                return jnp.concatenate([cols_of, mi_t], axis=0)

            def decode(rows):
                len_b = rows[:own_cols].T.astype(f32)
                return len_b, rows[own_cols:own_cols + kept].T.astype(jnp.int32)
        else:
            inside = (columns[None, :] >= path_start[:, None]) & (columns[None, :] < path_end[:, None])
            lengths = jnp.where(inside, seg_len, jnp.zeros_like(seg_len))

            def small_for(target):
                cols_of = lax.dynamic_slice_in_dim(lengths, target * own_cols, own_cols, axis=1)
                flat = jnp.concatenate([cols_of.reshape(-1), mode_index.astype(bf16).reshape(-1)])
                return pack_rows(flat, width)

            def decode(rows):
                flat = rows.reshape(-1)
                len_b = flat[:n_len].reshape(path_rows, own_cols).astype(f32)
                return len_b, flat[n_len:n_len + n_mi].reshape(path_rows, kept).astype(jnp.int32)

        scaled = (panels.astype(f32) * model.astype(f32)[:, None, :]).astype(bf16)
        scaled = scaled.reshape(own_cols * modes, depth_half)

        if split:
            own_off = c_idx * width
            other_off = (1 - c_idx) * width
            offsets = [own_off, other_off]
            mine = lax.dynamic_slice_in_dim(depth_weight, own_off, width, axis=1)
            theirs = lax.dynamic_slice_in_dim(depth_weight, other_off, width, axis=1)
            head = [mine]
        else:
            offsets = [0]
            head = [depth_weight]
        blocks = [(head + ([theirs] if split else []), small_for(p_idx))]
        sources = [p_idx]
        pairwise = n_paths & (n_paths - 1) == 0
        for k in reversed(range(1, n_paths)):
            if pairwise:
                target = source = p_idx ^ k
                perm = [(i, i ^ k) for i in range(n_paths)]
            else:
                target = (p_idx + k) % n_paths
                source = (p_idx - k) % n_paths
                perm = [(i, (i + k) % n_paths) for i in range(n_paths)]
            payload = jnp.concatenate([head[0], small_for(target)], axis=0)
            got = lax.ppermute(payload, "paths", perm)
            part_rows = got[:path_rows]
            dw_parts = [part_rows]
            if split:
                dw_parts.append(lax.ppermute(part_rows, "cols", [(0, 1), (1, 0)]))
            blocks.append((dw_parts, got[path_rows:]))
            sources.append(source)
        scaled_parts = [lax.dynamic_slice_in_dim(scaled, off, width, axis=1) for off in offsets]
        mode_ids = lax.iota(jnp.int32, modes)

        unpacked = []
        parts = []
        for s, (dw_parts, sm) in enumerate(blocks):
            len_own, mi_b = decode(sm)
            one_hot = (mi_b[:, :, None] == mode_ids[None, None, :]).astype(f32)
            unpacked.append((dw_parts, len_own, one_hot))
            part = None
            for dw_part, sc_part in zip(dw_parts, scaled_parts):
                weighted = lax.dot_general(
                    dw_part, sc_part, (((1,), (1,)), ((), ())), preferred_element_type=f32
                ).reshape(path_rows, own_cols, modes)
                per_mode = jnp.sum(len_own[:, :, None] * weighted, axis=1)
                term = jnp.sum(one_hot * per_mode[:, None, :], axis=2)
                part = term if part is None else part + term
            parts.append(part.T)
        first = (c_idx == 0) & (d_idx == 0)
        parts[0] = parts[0] - jnp.where(first, observed.T, jnp.zeros_like(observed.T))
        canon = jnp.zeros((n_paths,) + parts[0].shape, f32)
        for piece, source in zip(parts, sources):
            canon = lax.dynamic_update_index_in_dim(canon, piece, source, 0)

        local = n_cols * n_depth
        misfit_all = exchange_sum(canon, ("cols", "depth"), local)
        misfit_all = exchange_sum(misfit_all, "paths", n_paths)
        misfit = lax.dynamic_index_in_dim(misfit_all, p_idx, 0, keepdims=False).T
        rev = list(range(n_paths))
        mis_rows = jnp.concatenate(
            [lax.dynamic_index_in_dim(misfit_all, src, 0, keepdims=False).T for src in sources], axis=0
        )
        len_all = jnp.concatenate([unpacked[s][1] for s in rev], axis=0)
        hot_all = jnp.concatenate([unpacked[s][2] for s in rev], axis=0)
        resid = jnp.sum(mis_rows[:, :, None] * hot_all, axis=1)
        spread = (len_all[:, :, None] * resid[:, None, :]).astype(bf16)
        spread = spread.reshape(n_paths * path_rows, own_cols * modes)
        summed = []
        for j in range(len(offsets)):
            dw_all = jnp.concatenate([unpacked[s][0][j] for s in rev], axis=0)
            summed.append(
                lax.dot_general(
                    spread, dw_all, (((0,), (0,)), ((), ())), preferred_element_type=f32
                )
            )
        grads = []
        for acc, off in zip(summed, offsets):
            panel_part = lax.dynamic_slice_in_dim(panels, off, width, axis=2).astype(f32)
            grads.append(jnp.sum(acc.reshape(own_cols, modes, width) * panel_part, axis=1))
        gradient = jnp.zeros((own_cols, depth_half), f32)
        for g, off in zip(grads, offsets):
            gradient = lax.dynamic_update_slice_in_dim(gradient, g, off, axis=1)
        return (gradient, misfit)

    return shards


def solution(mesh):
    shards = make_shards(mesh.shape["paths"], mesh.shape["cols"], mesh.shape["depth"])
    return jax.shard_map(
        shards,
        mesh=mesh,
        in_specs=(
            P(("groups", "cols", "paths"), None, "depth"),
            P(("groups", "cols", "paths"), "depth"),
            P(("groups", "paths"), "depth"),
            P(("groups", "paths"), "cols"),
            P(("groups", "paths")),
            P(("groups", "paths")),
            P(("groups", "paths"), None),
            P(("groups", "paths"), None),
        ),
        out_specs=(P(("groups", "cols", "paths"), "depth"), P(("groups", "paths"), None)),
        check_vma=False,
    )
```

```python
import jax
import jax.numpy as jnp
from jax import lax
from jax.sharding import PartitionSpec as P

def shifted_copies(x, axes, count):
    copies = [x]
    for shift in range(1, count):
        perm = [(i, (i + shift) % count) for i in range(count)]
        copies.append(lax.ppermute(x, axes, perm))
    return copies


def place_by_source(copies, me, count):
    stacked = jnp.zeros((count,) + copies[0].shape, copies[0].dtype)
    for shift, piece in enumerate(copies):
        stacked = lax.dynamic_update_index_in_dim(stacked, piece, (me - shift) % count, 0)
    return stacked


def exchange_sum(x, axes, count):
    me = lax.axis_index(axes)
    if count & (count - 1):
        return jnp.sum(place_by_source(shifted_copies(x, axes, count), me, count), axis=0)
    stacked = jnp.zeros((count,) + x.shape, x.dtype)
    stacked = lax.dynamic_update_index_in_dim(stacked, x, me, 0)
    for k in reversed(range(1, count)):
        got = lax.ppermute(x, axes, [(i, i ^ k) for i in range(count)])
        stacked = lax.dynamic_update_index_in_dim(stacked, got, me ^ k, 0)
    return jnp.sum(stacked, axis=0)


def butterfly_sum(x, axes, count):
    step = 1
    while step < count:
        perm = [(i, i ^ step) for i in range(count)]
        x = x + lax.ppermute(x, axes, perm)
        step *= 2
    return x


def pack_rows(flat, width):
    pad = (-flat.shape[0]) % width
    return jnp.pad(flat, (0, pad)).reshape(-1, width)


def make_shards(n_paths, n_cols, n_depth):
    split = n_cols == 2

    def shards(panels, model, depth_weight, seg_len, path_start, path_end, mode_index, observed):
        own_cols, modes, depth_half = panels.shape
        path_rows, block_cols = seg_len.shape
        kept = mode_index.shape[1]
        f32, bf16 = jnp.float32, jnp.bfloat16
        p_idx = lax.axis_index("paths")
        c_idx = lax.axis_index("cols")
        d_idx = lax.axis_index("depth")

        columns = c_idx * block_cols + lax.iota(jnp.int32, block_cols)
        n_len = path_rows * own_cols
        n_mi = path_rows * kept
        if split:
            width = depth_half // 2
        else:
            width = depth_half
        if path_rows == width:
            inside_t = (columns[:, None] >= path_start[None, :]) & (columns[:, None] < path_end[None, :])
            seg_t = seg_len.T
            lengths_t = jnp.where(inside_t, seg_t, jnp.zeros_like(seg_t))
            mi_t = mode_index.T.astype(bf16)

            def small_for(target):
                cols_of = lax.dynamic_slice_in_dim(lengths_t, target * own_cols, own_cols, axis=0)
                return jnp.concatenate([cols_of, mi_t], axis=0)

            def decode(rows):
                len_b = rows[:own_cols].T.astype(f32)
                return len_b, rows[own_cols:own_cols + kept].T.astype(jnp.int32)
        else:
            inside = (columns[None, :] >= path_start[:, None]) & (columns[None, :] < path_end[:, None])
            lengths = jnp.where(inside, seg_len, jnp.zeros_like(seg_len))

            def small_for(target):
                cols_of = lax.dynamic_slice_in_dim(lengths, target * own_cols, own_cols, axis=1)
                flat = jnp.concatenate([cols_of.reshape(-1), mode_index.astype(bf16).reshape(-1)])
                return pack_rows(flat, width)

            def decode(rows):
                flat = rows.reshape(-1)
                len_b = flat[:n_len].reshape(path_rows, own_cols).astype(f32)
                return len_b, flat[n_len:n_len + n_mi].reshape(path_rows, kept).astype(jnp.int32)

        scaled = (panels.astype(f32) * model.astype(f32)[:, None, :]).astype(bf16)
        scaled = scaled.reshape(own_cols * modes, depth_half)

        if split:
            own_off = c_idx * width
            other_off = (1 - c_idx) * width
            offsets = [own_off, other_off]
            mine = lax.dynamic_slice_in_dim(depth_weight, own_off, width, axis=1)
            theirs = lax.dynamic_slice_in_dim(depth_weight, other_off, width, axis=1)
            head = [mine]
        else:
            offsets = [0]
            head = [depth_weight]
        blocks = [(head + ([theirs] if split else []), small_for(p_idx))]
        sources = [p_idx]
        pairwise = n_paths & (n_paths - 1) == 0
        for k in reversed(range(1, n_paths)):
            if pairwise:
                target = source = p_idx ^ k
                perm = [(i, i ^ k) for i in range(n_paths)]
            else:
                target = (p_idx + k) % n_paths
                source = (p_idx - k) % n_paths
                perm = [(i, (i + k) % n_paths) for i in range(n_paths)]
            payload = jnp.concatenate([head[0], small_for(target)], axis=0)
            got = lax.ppermute(payload, "paths", perm)
            part_rows = got[:path_rows]
            dw_parts = [part_rows]
            if split:
                dw_parts.append(lax.ppermute(part_rows, "cols", [(0, 1), (1, 0)]))
            blocks.append((dw_parts, got[path_rows:]))
            sources.append(source)
        scaled_parts = [lax.dynamic_slice_in_dim(scaled, off, width, axis=1) for off in offsets]
        mode_ids = lax.iota(jnp.int32, modes)

        unpacked = []
        parts = []
        for s, (dw_parts, sm) in enumerate(blocks):
            len_own, mi_b = decode(sm)
            one_hot = (mi_b[:, :, None] == mode_ids[None, None, :]).astype(f32)
            unpacked.append((dw_parts, len_own, one_hot))
            part = None
            for dw_part, sc_part in zip(dw_parts, scaled_parts):
                weighted = lax.dot_general(
                    dw_part, sc_part, (((1,), (1,)), ((), ())), preferred_element_type=f32
                ).reshape(path_rows, own_cols, modes)
                per_mode = jnp.sum(len_own[:, :, None] * weighted, axis=1)
                term = jnp.sum(one_hot * per_mode[:, None, :], axis=2)
                part = term if part is None else part + term
            parts.append(part.T)
        first = (c_idx == 0) & (d_idx == 0)
        parts[0] = parts[0] - jnp.where(first, observed.T, jnp.zeros_like(observed.T))
        canon = jnp.zeros((n_paths,) + parts[0].shape, f32)
        for piece, source in zip(parts, sources):
            canon = lax.dynamic_update_index_in_dim(canon, piece, source, 0)

        local = n_cols * n_depth
        misfit_all = exchange_sum(canon, ("cols", "depth"), local)
        misfit_all = exchange_sum(misfit_all, "paths", n_paths)
        misfit = lax.dynamic_index_in_dim(misfit_all, p_idx, 0, keepdims=False).T
        rev = list(range(n_paths))
        mis_rows = jnp.concatenate(
            [lax.dynamic_index_in_dim(misfit_all, src, 0, keepdims=False).T for src in sources], axis=0
        )
        len_all = jnp.concatenate([unpacked[s][1] for s in rev], axis=0)
        hot_all = jnp.concatenate([unpacked[s][2] for s in rev], axis=0)
        resid = jnp.sum(mis_rows[:, :, None] * hot_all, axis=1)
        spread = (len_all[:, :, None] * resid[:, None, :]).astype(bf16)
        spread = spread.reshape(n_paths * path_rows, own_cols * modes)
        summed = []
        for j in range(len(offsets)):
            dw_all = jnp.concatenate([unpacked[s][0][j] for s in rev], axis=0)
            summed.append(
                lax.dot_general(
                    spread, dw_all, (((0,), (0,)), ((), ())), preferred_element_type=f32
                )
            )
        grads = []
        for acc, off in zip(summed, offsets):
            panel_part = lax.dynamic_slice_in_dim(panels, off, width, axis=2).astype(f32)
            grads.append(jnp.sum(acc.reshape(own_cols, modes, width) * panel_part, axis=1))
        gradient = jnp.zeros((own_cols, depth_half), f32)
        for g, off in zip(grads, offsets):
            gradient = lax.dynamic_update_slice_in_dim(gradient, g, off, axis=1)
        return (gradient, misfit)

    return shards


def solution(mesh):
    shards = make_shards(mesh.shape["paths"], mesh.shape["cols"], mesh.shape["depth"])
    return jax.shard_map(
        shards,
        mesh=mesh,
        in_specs=(
            P(("groups", "cols", "paths"), None, "depth"),
            P(("groups", "cols", "paths"), "depth"),
            P(("groups", "paths"), "depth"),
            P(("groups", "paths"), "cols"),
            P(("groups", "paths")),
            P(("groups", "paths")),
            P(("groups", "paths"), None),
            P(("groups", "paths"), None),
        ),
        out_specs=(P(("groups", "cols", "paths"), "depth"), P(("groups", "paths"), None)),
        check_vma=False,
    )
```
